512 devices in a mesh: depth: 32 (over y, x), lat: 16 (over z, core).
Axes of the slice: x: 4, y: 8, z: 8, core: 2. Of those that a mesh axis runs over, the one named last changes fastest.
Arguments:
- thermal_state: float32 [1024, 8, 2048], P('depth', None, 'lat'), may hold values from -5 to 5
- sideways_face_flux_factor: float32 [1024, 8, 2048], P('depth', None, 'lat'), may hold values from 1 to 10
- downward_face_flux_factor: float32 [1024, 8, 2048], P('depth', None, 'lat'), may hold values from 1 to 10
Outputs:
- final_temperature: float32 [1024, 8, 2048], P('depth', None, 'lat')
The draws below stay inside these ranges and needn't reach their ends.
All inputs are finite; a program needn't handle non-finite values.
Results may differ from the reference program's by a relative error of at most 0.0013.
Values sent between devices are 32-bit elements; how exact they have to be, the bound alone decides.
No kernel may reach another device: no remote copies, remote signals or barrier semaphores. Data moves between devices by JAX's collectives and lax.ppermute only.
A program may use at most 64 MiB of HBM per device.

```python
import math
import jax
import jax.numpy as jnp
from jax import lax

Y = 8
NZ = 1024
NX = 2048


def draw_thermal_state(key, part):
    rough_values = jax.random.normal(key, (NZ, Y, NX), jnp.float32)
    return jnp.clip(rough_values, -5.0, 5.0)


def steps_of(rng, extent, shards, smallest, top_value):
    def one(position, blocks):
        heights = jax.random.uniform(jax.random.fold_in(jax.random.fold_in(rng, 6), position), (blocks,), jnp.float32, smallest / len(shards), top_value / len(shards))
        return jnp.repeat(jnp.exp(heights), extent[position] // blocks).reshape((-1,) + (1,) * (len(extent) - position - 1))

    factor_of = one(*shards[0])
    for cut in shards[1:]:
        factor_of = factor_of * one(*cut)
    return factor_of


def setup_inputs(seed: int = 0) -> dict:
    arg_keys = jax.random.split(jax.random.key(seed), 4)
    return {
        "thermal_state": draw_thermal_state(jax.random.fold_in(arg_keys[3], 71), 0),
        "sideways_face_flux_factor": jnp.clip(jnp.exp(math.log(10.0) - 2.3025851 * jax.random.uniform(arg_keys[1], (NZ, Y, NX), jnp.float32) ** steps_of(arg_keys[1], (NZ, Y, NX), ((0, 32), (2, 16)), -0.2, 0.2)), 1.0, 10.0),
        "downward_face_flux_factor": jnp.clip(jnp.exp(math.log(10.0) - 2.3025851 * jax.random.uniform(arg_keys[2], (NZ, Y, NX), jnp.float32) ** steps_of(arg_keys[2], (NZ, Y, NX), ((0, 32), (2, 16)), -0.2, 0.2)), 1.0, 10.0),
    }


sideways_coupling_quotient = 20.0
ratio_z = 2000.0

def line_solve(conduct, right_side, ratio_value):
    lower_band = -ratio_value * conduct
    upper_band = -ratio_value * jnp.concatenate([conduct[..., 1:], jnp.zeros_like(conduct[..., :1])], axis=-1)
    diagonal = 1.0 - lower_band - upper_band
    solve_lower = jnp.concatenate([jnp.zeros_like(lower_band[..., :1]), lower_band[..., 1:]], axis=-1)
    solved = lax.linalg.tridiagonal_solve(solve_lower, diagonal, upper_band, right_side[..., None])
    return solved[..., 0]

def reference(thermal_state, sideways_face_flux_factor, downward_face_flux_factor):
    extended_swapped_field = jnp.pad(thermal_state, ((0, 0), (0, 0), (1, 1)))
    source_vector_downward = jnp.pad(sideways_face_flux_factor, ((0, 0), (0, 0), (0, 1)))[:, :, 1:]
    known_operator_term = thermal_state + sideways_coupling_quotient * (source_vector_downward * (extended_swapped_field[:, :, 2:] - thermal_state) - sideways_face_flux_factor * (thermal_state - extended_swapped_field[:, :, :-2]))
    half_step = jnp.moveaxis(line_solve(jnp.moveaxis(downward_face_flux_factor, 0, -1), jnp.moveaxis(known_operator_term, 0, -1), ratio_z), -1, 0)
    reflected = 2.0 * half_step - known_operator_term
    final_step = line_solve(sideways_face_flux_factor, reflected, sideways_coupling_quotient)
    return final_step
```

```python
import jax
import jax.numpy as jnp
from jax import lax
from jax.sharding import PartitionSpec as P

sideways_coupling_quotient = 20.0
ratio_z = 2000.0


def take_rows(values, start, stop, axis_index):
    return lax.slice_in_dim(values, start, stop, axis=axis_index)


def moved(values, stride, axis_index, filler, forward):
    count = values.shape[axis_index]
    pad_shape = list(values.shape)
    pad_shape[axis_index] = stride
    padding = jnp.full(pad_shape, filler, values.dtype)
    if forward:
        return jnp.concatenate(
            [take_rows(values, stride, count, axis_index), padding], axis=axis_index
        )
    return jnp.concatenate(
        [padding, take_rows(values, 0, count - stride, axis_index)], axis=axis_index
    )


def level_update(lower_band, diagonal, upper_band, rights, below, above):
    alpha_term = -lower_band / below[1]
    gamma_term = -upper_band / above[1]
    new_diagonal = diagonal + alpha_term * below[2] + gamma_term * above[0]
    new_rights = tuple(
        (
            column + alpha_term * low_col + gamma_term * high_col
            for column, low_col, high_col in zip(rights, below[3], above[3])
        )
    )
    return (alpha_term * below[0], new_diagonal, gamma_term * above[2], new_rights)


def cyclic(lower_band, diagonal, upper_band, rights, axis_index):
    count = lower_band.shape[axis_index]
    stride = 1
    while stride < count:
        below = (
            moved(lower_band, stride, axis_index, 0.0, False),
            moved(diagonal, stride, axis_index, 1.0, False),
            moved(upper_band, stride, axis_index, 0.0, False),
            tuple((moved(column, stride, axis_index, 0.0, False) for column in rights)),
        )
        above = (
            moved(lower_band, stride, axis_index, 0.0, True),
            moved(diagonal, stride, axis_index, 1.0, True),
            moved(upper_band, stride, axis_index, 0.0, True),
            tuple((moved(column, stride, axis_index, 0.0, True) for column in rights)),
        )
        lower_band, diagonal, upper_band, rights = level_update(
            lower_band, diagonal, upper_band, rights, below, above
        )
        stride = stride * 2
    return tuple((column / diagonal for column in rights))


def gathered(values, axis):
    count = lax.axis_size(axis)
    copies = jnp.broadcast_to(values[None], (count,) + values.shape)
    return lax.all_to_all(copies, axis, 0, 0, tiled=False)


def partition_solve(conduct, first_next, rights, ratio, axis_index, axis):
    count = conduct.shape[axis_index]
    lower_band = -ratio * conduct
    inner_lower = take_rows(lower_band, 0, count - 1, axis_index)
    upper_inner = -ratio * take_rows(conduct, 1, count, axis_index)
    diagonal = 1.0 - inner_lower - upper_inner
    positions = lax.broadcasted_iota(jnp.int32, inner_lower.shape, axis_index)
    first_lower = take_rows(inner_lower, 0, 1, axis_index)
    last_upper = take_rows(upper_inner, count - 2, count - 1, axis_index)
    solve_lower = jnp.where(positions == 0, 0.0, inner_lower)
    solve_upper = jnp.where(positions == count - 2, 0.0, upper_inner)
    from_prev = jnp.where(positions == 0, -first_lower, 0.0)
    from_next = jnp.where(positions == count - 2, -last_upper, 0.0)
    inner_rights = take_rows(rights, 0, count - 1, axis_index)
    local_part, prev_part, next_part = cyclic(
        solve_lower, diagonal, solve_upper, (inner_rights, from_prev, from_next), axis_index
    )
    tail_local = take_rows(local_part, count - 2, count - 1, axis_index)
    tail_prev = take_rows(prev_part, count - 2, count - 1, axis_index)
    tail_next = take_rows(next_part, count - 2, count - 1, axis_index)
    lower_last = take_rows(lower_band, count - 1, count, axis_index)
    right_last = take_rows(rights, count - 1, count, axis_index)
    pieces = jnp.stack(
        [
            lower_last * tail_prev,
            1.0 - lower_last + lower_last * tail_next,
            right_last - lower_last * tail_local,
            take_rows(local_part, 0, 1, axis_index),
            take_rows(prev_part, 0, 1, axis_index),
            take_rows(next_part, 0, 1, axis_index),
            take_rows(conduct, 0, 1, axis_index),
        ]
    )
    line_shape = pieces.shape[1:]
    flat = pieces.reshape(7, -1)
    every = gathered(flat, axis)
    blocks = every.shape[0]
    own_lower, own_diag, own_right = every[:, 0], every[:, 1], every[:, 2]
    zero_row = jnp.zeros_like(every[:1, 0])
    next_heads = [
        jnp.concatenate([every[1:, i], zero_row], axis=0) for i in (3, 4, 5, 6)
    ]
    head_local, head_prev, head_next, next_conduct = next_heads
    coupling = -ratio * next_conduct
    red_diag = own_diag - coupling + coupling * head_prev
    red_upper = coupling * head_next
    red_right = own_right - coupling * head_local
    solved = cyclic(own_lower, red_diag, red_upper, (red_right,), 0)[0]
    padded = jnp.concatenate([zero_row, solved], axis=0)
    index = lax.axis_index(axis)
    previous = lax.dynamic_slice_in_dim(padded, index, 1, 0).reshape(line_shape)
    interface_value = lax.dynamic_slice_in_dim(padded, index + 1, 1, 0).reshape(line_shape)
    inner_values = local_part + prev_part * previous + next_part * interface_value
    del blocks, first_next
    return jnp.concatenate([inner_values, interface_value], axis=axis_index)


def on_device(thermal_state, sideways_face_flux_factor, downward_face_flux_factor):
    width = thermal_state.shape[2]
    count = lax.axis_size("lat")
    right_pairs = [(i, i + 1) for i in range(count - 1)]
    left_pairs = [(i + 1, i) for i in range(count - 1)]
    first_cols = jnp.stack(
        [thermal_state[:, :, :1], sideways_face_flux_factor[:, :, :1]]
    )
    from_right = lax.ppermute(first_cols, "lat", left_pairs)
    from_left = lax.ppermute(thermal_state[:, :, width - 1 :], "lat", right_pairs)
    temp_right = jnp.concatenate([thermal_state[:, :, 1:], from_right[0]], axis=2)
    conduct_right = jnp.concatenate(
        [sideways_face_flux_factor[:, :, 1:], from_right[1]], axis=2
    )
    temp_left = jnp.concatenate([from_left, thermal_state[:, :, : width - 1]], axis=2)
    known_operator_term = thermal_state + sideways_coupling_quotient * (
        conduct_right * (temp_right - thermal_state)
        - sideways_face_flux_factor * (thermal_state - temp_left)
    )
    half_step = partition_solve(
        downward_face_flux_factor, None, known_operator_term, ratio_z, 0, "depth"
    )
    reflected = 2.0 * half_step - known_operator_term
    return partition_solve(
        sideways_face_flux_factor, None, reflected, sideways_coupling_quotient, 2, "lat"
    )


def solution(mesh):
    in_specs = (P("depth", None, "lat"), P("depth", None, "lat"), P("depth", None, "lat"))
    out_specs = P("depth", None, "lat")
    return jax.shard_map(
        on_device, mesh=mesh, in_specs=in_specs, out_specs=out_specs, check_vma=False
    )
```

```python
import jax
import jax.numpy as jnp
from jax import lax
from jax.sharding import PartitionSpec as P
from jax.experimental import pallas as pl
from jax.experimental.pallas import tpu as pltpu

sideways_coupling_quotient = 20.0
ratio_z = 2000.0


def take_rows(values, start, stop, axis_index):
    return lax.slice_in_dim(values, start, stop, axis=axis_index)


def moved(values, stride, axis_index, filler, forward):
    count = values.shape[axis_index]
    pad_shape = list(values.shape)
    pad_shape[axis_index] = stride
    padding = jnp.full(pad_shape, filler, values.dtype)
    if forward:
        return jnp.concatenate(
            [take_rows(values, stride, count, axis_index), padding], axis=axis_index
        )
    return jnp.concatenate(
        [padding, take_rows(values, 0, count - stride, axis_index)], axis=axis_index
    )


def level_update(lower_band, diagonal, upper_band, rights, below, above):
    alpha_term = -lower_band / below[1]
    gamma_term = -upper_band / above[1]
    new_diagonal = diagonal + alpha_term * below[2] + gamma_term * above[0]
    new_rights = tuple(
        (
            column + alpha_term * low_col + gamma_term * high_col
            for column, low_col, high_col in zip(rights, below[3], above[3])
        )
    )
    return (alpha_term * below[0], new_diagonal, gamma_term * above[2], new_rights)


def cyclic(lower_band, diagonal, upper_band, rights, axis_index):
    count = lower_band.shape[axis_index]
    stride = 1
    while stride < count:
        below = (
            moved(lower_band, stride, axis_index, 0.0, False),
            moved(diagonal, stride, axis_index, 1.0, False),
            moved(upper_band, stride, axis_index, 0.0, False),
            tuple((moved(column, stride, axis_index, 0.0, False) for column in rights)),
        )
        above = (
            moved(lower_band, stride, axis_index, 0.0, True),
            moved(diagonal, stride, axis_index, 1.0, True),
            moved(upper_band, stride, axis_index, 0.0, True),
            tuple((moved(column, stride, axis_index, 0.0, True) for column in rights)),
        )
        lower_band, diagonal, upper_band, rights = level_update(
            lower_band, diagonal, upper_band, rights, below, above
        )
        stride = stride * 2
    return tuple((column / diagonal for column in rights))


def gathered(values, axis):
    count = lax.axis_size(axis)
    copies = jnp.broadcast_to(values[None], (count,) + values.shape)
    return lax.all_to_all(copies, axis, 0, 0, tiled=False)


def depth_kernel(t_ref, s_ref, d_ref, tr_ref, sr_ref, tl_ref, base_ref, p_ref, n_ref, pieces_ref):
    rows, _, width = t_ref.shape
    temp = t_ref[...]
    conduct = s_ref[...]
    lane = lax.broadcasted_iota(jnp.int32, temp.shape, 2)
    last = lane == width - 1
    first = lane == 0
    temp_right = jnp.where(last, tr_ref[...], pltpu.roll(temp, width - 1, 2))
    conduct_right = jnp.where(last, sr_ref[...], pltpu.roll(conduct, width - 1, 2))
    temp_left = jnp.where(first, tl_ref[...], pltpu.roll(temp, 1, 2))
    base_ref[...] = temp + sideways_coupling_quotient * (
        conduct_right * (temp_right - temp) - conduct * (temp - temp_left)
    )
    inner = rows - 1
    lower = [-ratio_z * d_ref[i] for i in range(rows)]
    upper = [lower[i + 1] for i in range(inner)]
    c_term, r_local, r_prev = [], [], []
    r_next = None
    for i in range(inner):
        diagonal = 1.0 - lower[i] - upper[i]
        rhs = base_ref[i]
        if i == 0:
            den = diagonal
            local = rhs / den
            prev = -lower[i] / den
        else:
            den = diagonal - lower[i] * c_term[i - 1]
            local = (rhs - lower[i] * r_local[i - 1]) / den
            prev = (-lower[i] * r_prev[i - 1]) / den
        if i < inner - 1:
            c_term.append(upper[i] / den)
        else:
            c_term.append(None)
            r_next = -upper[i] / den
        r_local.append(local)
        r_prev.append(prev)
    local = r_local[inner - 1]
    prev = r_prev[inner - 1]
    nxt = r_next
    lower_last = lower[rows - 1]
    right_last = base_ref[rows - 1]
    pieces_ref[0] = lower_last * prev
    pieces_ref[1] = 1.0 - lower_last + lower_last * nxt
    pieces_ref[2] = right_last - lower_last * local
    base_ref[rows - 1] = -right_last
    p_ref[rows - 1] = jnp.zeros_like(local)
    n_ref[rows - 1] = jnp.full_like(local, 2.0)
    for i in range(inner - 1, -1, -1):
        if i < inner - 1:
            local = r_local[i] - c_term[i] * local
            prev = r_prev[i] - c_term[i] * prev
            nxt = -c_term[i] * nxt
        base_ref[i] = 2.0 * local - base_ref[i]
        p_ref[i] = 2.0 * prev
        n_ref[i] = 2.0 * nxt
    pieces_ref[3] = local
    pieces_ref[4] = prev
    pieces_ref[5] = nxt
    pieces_ref[6] = d_ref[0]


def depth_local(temp, conduct, downward, temp_next, conduct_next, temp_prev):
    rows, lines, width = temp.shape
    full = jax.ShapeDtypeStruct(temp.shape, temp.dtype)
    return pl.pallas_call(
        depth_kernel,
        out_shape=(full, full, full, jax.ShapeDtypeStruct((7, lines, width), temp.dtype)),
    )(temp, conduct, downward, temp_next, conduct_next, temp_prev)


def reduced_solve(pieces, ratio, axis):
    line_shape = pieces.shape[1:]
    every = gathered(pieces.reshape(7, -1), axis)
    own_lower, own_diag, own_right = every[:, 0], every[:, 1], every[:, 2]
    zero_row = jnp.zeros_like(every[:1, 0])
    next_heads = [
        jnp.concatenate([every[1:, i], zero_row], axis=0) for i in (3, 4, 5, 6)
    ]
    head_local, head_prev, head_next, next_conduct = next_heads
    coupling = -ratio * next_conduct
    red_diag = own_diag - coupling + coupling * head_prev
    red_upper = coupling * head_next
    red_right = own_right - coupling * head_local
    solved = cyclic(own_lower, red_diag, red_upper, (red_right,), 0)[0]
    padded = jnp.concatenate([zero_row, solved], axis=0)
    index = lax.axis_index(axis)
    previous = lax.dynamic_slice_in_dim(padded, index, 1, 0).reshape(line_shape)
    interface_value = lax.dynamic_slice_in_dim(padded, index + 1, 1, 0).reshape(line_shape)
    return previous, interface_value


def partition_solve(conduct, first_next, rights, ratio, axis_index, axis):
    count = conduct.shape[axis_index]
    lower_band = -ratio * conduct
    inner_lower = take_rows(lower_band, 0, count - 1, axis_index)
    upper_inner = -ratio * take_rows(conduct, 1, count, axis_index)
    diagonal = 1.0 - inner_lower - upper_inner
    positions = lax.broadcasted_iota(jnp.int32, inner_lower.shape, axis_index)
    first_lower = take_rows(inner_lower, 0, 1, axis_index)
    last_upper = take_rows(upper_inner, count - 2, count - 1, axis_index)
    solve_lower = jnp.where(positions == 0, 0.0, inner_lower)
    solve_upper = jnp.where(positions == count - 2, 0.0, upper_inner)
    from_prev = jnp.where(positions == 0, -first_lower, 0.0)
    from_next = jnp.where(positions == count - 2, -last_upper, 0.0)
    inner_rights = take_rows(rights, 0, count - 1, axis_index)
    local_part, prev_part, next_part = cyclic(
        solve_lower, diagonal, solve_upper, (inner_rights, from_prev, from_next), axis_index
    )
    tail_local = take_rows(local_part, count - 2, count - 1, axis_index)
    tail_prev = take_rows(prev_part, count - 2, count - 1, axis_index)
    tail_next = take_rows(next_part, count - 2, count - 1, axis_index)
    lower_last = take_rows(lower_band, count - 1, count, axis_index)
    right_last = take_rows(rights, count - 1, count, axis_index)
    pieces = jnp.stack(
        [
            lower_last * tail_prev,
            1.0 - lower_last + lower_last * tail_next,
            right_last - lower_last * tail_local,
            take_rows(local_part, 0, 1, axis_index),
            take_rows(prev_part, 0, 1, axis_index),
            take_rows(next_part, 0, 1, axis_index),
            take_rows(conduct, 0, 1, axis_index),
        ]
    )
    line_shape = pieces.shape[1:]
    flat = pieces.reshape(7, -1)
    every = gathered(flat, axis)
    blocks = every.shape[0]
    own_lower, own_diag, own_right = every[:, 0], every[:, 1], every[:, 2]
    zero_row = jnp.zeros_like(every[:1, 0])
    next_heads = [
        jnp.concatenate([every[1:, i], zero_row], axis=0) for i in (3, 4, 5, 6)
    ]
    head_local, head_prev, head_next, next_conduct = next_heads
    coupling = -ratio * next_conduct
    red_diag = own_diag - coupling + coupling * head_prev
    red_upper = coupling * head_next
    red_right = own_right - coupling * head_local
    solved = cyclic(own_lower, red_diag, red_upper, (red_right,), 0)[0]
    padded = jnp.concatenate([zero_row, solved], axis=0)
    index = lax.axis_index(axis)
    previous = lax.dynamic_slice_in_dim(padded, index, 1, 0).reshape(line_shape)
    interface_value = lax.dynamic_slice_in_dim(padded, index + 1, 1, 0).reshape(line_shape)
    inner_values = local_part + prev_part * previous + next_part * interface_value
    del blocks, first_next
    return jnp.concatenate([inner_values, interface_value], axis=axis_index)


def on_device(thermal_state, sideways_face_flux_factor, downward_face_flux_factor):
    width = thermal_state.shape[2]
    count = lax.axis_size("lat")
    right_pairs = [(i, i + 1) for i in range(count - 1)]
    left_pairs = [(i + 1, i) for i in range(count - 1)]
    first_cols = jnp.stack(
        [thermal_state[:, :, :1], sideways_face_flux_factor[:, :, :1]]
    )
    from_right = lax.ppermute(first_cols, "lat", left_pairs)
    from_left = lax.ppermute(thermal_state[:, :, width - 1 :], "lat", right_pairs)
    base, prev_weight, own_weight, pieces = depth_local(
        thermal_state,
        sideways_face_flux_factor,
        downward_face_flux_factor,
        from_right[0],
        from_right[1],
        from_left,
    )
    previous, interface_value = reduced_solve(pieces, ratio_z, "depth")
    reflected = base + prev_weight * previous + own_weight * interface_value
    return partition_solve(
        sideways_face_flux_factor, None, reflected, sideways_coupling_quotient, 2, "lat"
    )


def solution(mesh):
    in_specs = (P("depth", None, "lat"), P("depth", None, "lat"), P("depth", None, "lat"))
    out_specs = P("depth", None, "lat")
    return jax.shard_map(
        on_device, mesh=mesh, in_specs=in_specs, out_specs=out_specs, check_vma=False
    )
```

```python
import jax
import jax.numpy as jnp
from jax import lax
from jax.sharding import PartitionSpec as P
from jax.experimental import pallas as pl
from jax.experimental.pallas import tpu as pltpu

sideways_coupling_quotient = 20.0
ratio_z = 2000.0


def take_rows(values, start, stop, axis_index):
    return lax.slice_in_dim(values, start, stop, axis=axis_index)


def moved(values, stride, axis_index, filler, forward):
    count = values.shape[axis_index]
    pad_shape = list(values.shape)
    pad_shape[axis_index] = stride
    padding = jnp.full(pad_shape, filler, values.dtype)
    if forward:
        return jnp.concatenate(
            [take_rows(values, stride, count, axis_index), padding], axis=axis_index
        )
    return jnp.concatenate(
        [padding, take_rows(values, 0, count - stride, axis_index)], axis=axis_index
    )


def level_update(lower_band, diagonal, upper_band, rights, below, above):
    alpha_term = -lower_band / below[1]
    gamma_term = -upper_band / above[1]
    new_diagonal = diagonal + alpha_term * below[2] + gamma_term * above[0]
    new_rights = tuple(
        (
            column + alpha_term * low_col + gamma_term * high_col
            for column, low_col, high_col in zip(rights, below[3], above[3])
        )
    )
    return (alpha_term * below[0], new_diagonal, gamma_term * above[2], new_rights)


def cyclic(lower_band, diagonal, upper_band, rights, axis_index):
    count = lower_band.shape[axis_index]
    stride = 1
    while stride < count:
        below = (
            moved(lower_band, stride, axis_index, 0.0, False),
            moved(diagonal, stride, axis_index, 1.0, False),
            moved(upper_band, stride, axis_index, 0.0, False),
            tuple((moved(column, stride, axis_index, 0.0, False) for column in rights)),
        )
        above = (
            moved(lower_band, stride, axis_index, 0.0, True),
            moved(diagonal, stride, axis_index, 1.0, True),
            moved(upper_band, stride, axis_index, 0.0, True),
            tuple((moved(column, stride, axis_index, 0.0, True) for column in rights)),
        )
        lower_band, diagonal, upper_band, rights = level_update(
            lower_band, diagonal, upper_band, rights, below, above
        )
        stride = stride * 2
    return tuple((column / diagonal for column in rights))


def depth_kernel(t_ref, s_ref, d_ref, tr_ref, sr_ref, tl_ref, base_ref, p_ref, n_ref, pieces_ref):
    rows, _, width = t_ref.shape
    temp = t_ref[...]
    conduct = s_ref[...]
    lane = lax.broadcasted_iota(jnp.int32, temp.shape, 2)
    last = lane == width - 1
    first = lane == 0
    temp_right = jnp.where(last, tr_ref[...], pltpu.roll(temp, width - 1, 2))
    conduct_right = jnp.where(last, sr_ref[...], pltpu.roll(conduct, width - 1, 2))
    temp_left = jnp.where(first, tl_ref[...], pltpu.roll(temp, 1, 2))
    base_ref[...] = temp + sideways_coupling_quotient * (
        conduct_right * (temp_right - temp) - conduct * (temp - temp_left)
    )
    inner = rows - 1
    lower = [-ratio_z * d_ref[i] for i in range(rows)]
    upper = [lower[i + 1] for i in range(inner)]
    c_term, r_local, r_prev = [], [], []
    r_next = None
    for i in range(inner):
        diagonal = 1.0 - lower[i] - upper[i]
        rhs = base_ref[i]
        if i == 0:
            den = diagonal
            local = rhs / den
            prev = -lower[i] / den
        else:
            den = diagonal - lower[i] * c_term[i - 1]
            local = (rhs - lower[i] * r_local[i - 1]) / den
            prev = (-lower[i] * r_prev[i - 1]) / den
        if i < inner - 1:
            c_term.append(upper[i] / den)
        else:
            c_term.append(None)
            r_next = -upper[i] / den
        r_local.append(local)
        r_prev.append(prev)
    local = r_local[inner - 1]
    prev = r_prev[inner - 1]
    nxt = r_next
    lower_last = lower[rows - 1]
    right_last = base_ref[rows - 1]
    own_lower = lower_last * prev
    own_diag = 1.0 - lower_last + lower_last * nxt
    own_right = right_last - lower_last * local
    base_ref[rows - 1] = -right_last
    p_ref[rows - 1] = jnp.zeros_like(local)
    n_ref[rows - 1] = jnp.full_like(local, 2.0)
    for i in range(inner - 1, -1, -1):
        if i < inner - 1:
            local = r_local[i] - c_term[i] * local
            prev = r_prev[i] - c_term[i] * prev
            nxt = -c_term[i] * nxt
        base_ref[i] = 2.0 * local - base_ref[i]
        p_ref[i] = 2.0 * prev
        n_ref[i] = 2.0 * nxt
    head_coupling = lower[0]
    own = (
        own_lower,
        own_diag,
        own_right,
        head_coupling * (prev - 1.0),
        head_coupling * nxt,
        head_coupling * local,
    )
    for block in range(pieces_ref.shape[0]):
        for i in range(6):
            pieces_ref[block, i] = own[i]


def depth_local(temp, conduct, downward, temp_next, conduct_next, temp_prev, blocks):
    rows, lines, width = temp.shape
    full = jax.ShapeDtypeStruct(temp.shape, temp.dtype)
    copies = jax.ShapeDtypeStruct((blocks, 6, lines, width), temp.dtype)
    return pl.pallas_call(depth_kernel, out_shape=(full, full, full, copies))(temp, conduct, downward, temp_next, conduct_next, temp_prev)


def reduced_solve(copies, ratio, axis):
    line_shape = copies.shape[2:]
    flat = copies.reshape(copies.shape[:2] + (-1,))
    every = lax.all_to_all(flat, axis, 0, 0, tiled=False)
    zero_row = jnp.zeros_like(every[:1, 0])
    from_next = [jnp.concatenate([every[1:, i], zero_row], axis=0) for i in (3, 4, 5)]
    red_diag = every[:, 1] + from_next[0]
    red_upper = from_next[1]
    red_right = every[:, 2] - from_next[2]
    solved = cyclic(every[:, 0], red_diag, red_upper, (red_right,), 0)[0]
    padded = jnp.concatenate([zero_row, solved], axis=0)
    index = lax.axis_index(axis)
    previous = lax.dynamic_slice_in_dim(padded, index, 1, 0).reshape(line_shape)
    interface_value = lax.dynamic_slice_in_dim(padded, index + 1, 1, 0).reshape(line_shape)
    return previous, interface_value


def partition_solve(conduct, first_next, rights, ratio, axis_index, axis):
    count = conduct.shape[axis_index]
    lower_band = -ratio * conduct
    inner_lower = take_rows(lower_band, 0, count - 1, axis_index)
    upper_inner = -ratio * take_rows(conduct, 1, count, axis_index)
    diagonal = 1.0 - inner_lower - upper_inner
    positions = lax.broadcasted_iota(jnp.int32, inner_lower.shape, axis_index)
    first_lower = take_rows(inner_lower, 0, 1, axis_index)
    last_upper = take_rows(upper_inner, count - 2, count - 1, axis_index)
    solve_lower = jnp.where(positions == 0, 0.0, inner_lower)
    solve_upper = jnp.where(positions == count - 2, 0.0, upper_inner)
    from_prev = jnp.where(positions == 0, -first_lower, 0.0)
    from_next = jnp.where(positions == count - 2, -last_upper, 0.0)
    inner_rights = take_rows(rights, 0, count - 1, axis_index)
    local_part, prev_part, next_part = cyclic(
        solve_lower, diagonal, solve_upper, (inner_rights, from_prev, from_next), axis_index
    )
    tail_local = take_rows(local_part, count - 2, count - 1, axis_index)
    tail_prev = take_rows(prev_part, count - 2, count - 1, axis_index)
    tail_next = take_rows(next_part, count - 2, count - 1, axis_index)
    lower_last = take_rows(lower_band, count - 1, count, axis_index)
    right_last = take_rows(rights, count - 1, count, axis_index)
    head_coupling = take_rows(lower_band, 0, 1, axis_index)
    pieces = jnp.stack(
        [
            lower_last * tail_prev,
            1.0 - lower_last + lower_last * tail_next,
            right_last - lower_last * tail_local,
            head_coupling * (take_rows(prev_part, 0, 1, axis_index) - 1.0),
            head_coupling * take_rows(next_part, 0, 1, axis_index),
            head_coupling * take_rows(local_part, 0, 1, axis_index),
        ]
    )
    blocks = lax.axis_size(axis)
    copies = jnp.broadcast_to(pieces[None], (blocks,) + pieces.shape)
    previous, interface_value = reduced_solve(copies, ratio, axis)
    inner_values = local_part + prev_part * previous + next_part * interface_value
    return jnp.concatenate([inner_values, interface_value], axis=axis_index)


def on_device(thermal_state, sideways_face_flux_factor, downward_face_flux_factor):
    width = thermal_state.shape[2]
    count = lax.axis_size("lat")
    right_pairs = [(i, i + 1) for i in range(count - 1)]
    left_pairs = [(i + 1, i) for i in range(count - 1)]
    first_cols = jnp.stack(
        [thermal_state[:, :, :1], sideways_face_flux_factor[:, :, :1]]
    )
    from_right = lax.ppermute(first_cols, "lat", left_pairs)
    from_left = lax.ppermute(thermal_state[:, :, width - 1 :], "lat", right_pairs)
    base, prev_weight, own_weight, pieces = depth_local(
        thermal_state,
        sideways_face_flux_factor,
        downward_face_flux_factor,
        from_right[0],
        from_right[1],
        from_left,
        lax.axis_size("depth"),
    )
    previous, interface_value = reduced_solve(pieces, ratio_z, "depth")
    reflected = base + prev_weight * previous + own_weight * interface_value
    return partition_solve(
        sideways_face_flux_factor, None, reflected, sideways_coupling_quotient, 2, "lat"
    )


def solution(mesh):
    in_specs = (P("depth", None, "lat"), P("depth", None, "lat"), P("depth", None, "lat"))
    out_specs = P("depth", None, "lat")
    return jax.shard_map(
        on_device, mesh=mesh, in_specs=in_specs, out_specs=out_specs, check_vma=False
    )
```

```python
import jax
import jax.numpy as jnp
from jax import lax
from jax.sharding import PartitionSpec as P
from jax.experimental import pallas as pl
from jax.experimental.pallas import tpu as pltpu

sideways_coupling_quotient = 20.0
ratio_z = 2000.0


def take_rows(values, start, stop, axis_index):
    return lax.slice_in_dim(values, start, stop, axis=axis_index)


def moved(values, stride, axis_index, filler, forward):
    count = values.shape[axis_index]
    pad_shape = list(values.shape)
    pad_shape[axis_index] = stride
    padding = jnp.full(pad_shape, filler, values.dtype)
    if forward:
        return jnp.concatenate(
            [take_rows(values, stride, count, axis_index), padding], axis=axis_index
        )
    return jnp.concatenate(
        [padding, take_rows(values, 0, count - stride, axis_index)], axis=axis_index
    )


def level_update(lower_band, diagonal, upper_band, rights, below, above):
    alpha_term = -lower_band / below[1]
    gamma_term = -upper_band / above[1]
    new_diagonal = diagonal + alpha_term * below[2] + gamma_term * above[0]
    new_rights = tuple(
        (
            column + alpha_term * low_col + gamma_term * high_col
            for column, low_col, high_col in zip(rights, below[3], above[3])
        )
    )
    return (alpha_term * below[0], new_diagonal, gamma_term * above[2], new_rights)


def cyclic(lower_band, diagonal, upper_band, rights, axis_index):
    count = lower_band.shape[axis_index]
    stride = 1
    while stride < count:
        below = (
            moved(lower_band, stride, axis_index, 0.0, False),
            moved(diagonal, stride, axis_index, 1.0, False),
            moved(upper_band, stride, axis_index, 0.0, False),
            tuple((moved(column, stride, axis_index, 0.0, False) for column in rights)),
        )
        above = (
            moved(lower_band, stride, axis_index, 0.0, True),
            moved(diagonal, stride, axis_index, 1.0, True),
            moved(upper_band, stride, axis_index, 0.0, True),
            tuple((moved(column, stride, axis_index, 0.0, True) for column in rights)),
        )
        lower_band, diagonal, upper_band, rights = level_update(
            lower_band, diagonal, upper_band, rights, below, above
        )
        stride = stride * 2
    return tuple((column / diagonal for column in rights))


def depth_kernel(t_ref, s_ref, d_ref, right_ref, tl_ref, base_ref, p_ref, n_ref, pieces_ref):
    rows, _, width = t_ref.shape
    temp = t_ref[...]
    conduct = s_ref[...]
    lane = lax.broadcasted_iota(jnp.int32, temp.shape, 2)
    last = lane == width - 1
    first = lane == 0
    temp_right = jnp.where(last, right_ref[0], pltpu.roll(temp, width - 1, 2))
    conduct_right = jnp.where(last, right_ref[1], pltpu.roll(conduct, width - 1, 2))
    temp_left = jnp.where(first, tl_ref[...], pltpu.roll(temp, 1, 2))
    base_ref[...] = temp + sideways_coupling_quotient * (
        conduct_right * (temp_right - temp) - conduct * (temp - temp_left)
    )
    inner = rows - 1
    lower = [-ratio_z * d_ref[i] for i in range(rows)]
    upper = [lower[i + 1] for i in range(inner)]
    c_term, r_local, r_prev = [], [], []
    r_next = None
    for i in range(inner):
        diagonal = 1.0 - lower[i] - upper[i]
        rhs = base_ref[i]
        if i == 0:
            den = diagonal
            local = rhs / den
            prev = -lower[i] / den
        else:
            den = diagonal - lower[i] * c_term[i - 1]
            local = (rhs - lower[i] * r_local[i - 1]) / den
            prev = (-lower[i] * r_prev[i - 1]) / den
        if i < inner - 1:
            c_term.append(upper[i] / den)
        else:
            c_term.append(None)
            r_next = -upper[i] / den
        r_local.append(local)
        r_prev.append(prev)
    local = r_local[inner - 1]
    prev = r_prev[inner - 1]
    nxt = r_next
    lower_last = lower[rows - 1]
    right_last = base_ref[rows - 1]
    own_lower = lower_last * prev
    own_diag = 1.0 - lower_last + lower_last * nxt
    own_right = right_last - lower_last * local
    base_ref[rows - 1] = -right_last
    p_ref[rows - 1] = jnp.zeros_like(local)
    n_ref[rows - 1] = jnp.full_like(local, 2.0)
    for i in range(inner - 1, -1, -1):
        if i < inner - 1:
            local = r_local[i] - c_term[i] * local
            prev = r_prev[i] - c_term[i] * prev
            nxt = -c_term[i] * nxt
        base_ref[i] = 2.0 * local - base_ref[i]
        p_ref[i] = 2.0 * prev
        n_ref[i] = 2.0 * nxt
    head_coupling = lower[0]
    own = (
        own_lower,
        own_diag,
        own_right,
        head_coupling * (prev - 1.0),
        head_coupling * nxt,
        head_coupling * local,
    )
    for block in range(pieces_ref.shape[0]):
        for i in range(6):
            pieces_ref[block, i] = own[i]


def depth_local(temp, conduct, downward, from_right, temp_prev, blocks):
    rows, lines, width = temp.shape
    full = jax.ShapeDtypeStruct(temp.shape, temp.dtype)
    copies = jax.ShapeDtypeStruct((blocks, 6, lines, width), temp.dtype)
    return pl.pallas_call(depth_kernel, out_shape=(full, full, full, copies))(
        temp, conduct, downward, from_right, temp_prev
    )


def reduced_solve(copies, ratio, axis):
    line_shape = copies.shape[2:]
    every = lax.all_to_all(copies, axis, 0, 0, tiled=False)
    zero_row = jnp.zeros_like(every[:1, 0])
    from_next = [jnp.concatenate([every[1:, i], zero_row], axis=0) for i in (3, 4, 5)]
    red_diag = every[:, 1] + from_next[0]
    red_upper = from_next[1]
    red_right = every[:, 2] - from_next[2]
    solved = cyclic(every[:, 0], red_diag, red_upper, (red_right,), 0)[0]
    padded = jnp.concatenate([zero_row, solved], axis=0)
    index = lax.axis_index(axis)
    previous = lax.dynamic_slice_in_dim(padded, index, 1, 0)[0]
    interface_value = lax.dynamic_slice_in_dim(padded, index + 1, 1, 0)[0]
    return previous, interface_value


def partition_solve(conduct, first_next, rights, ratio, axis_index, axis):
    count = conduct.shape[axis_index]
    lower_band = -ratio * conduct
    inner_lower = take_rows(lower_band, 0, count - 1, axis_index)
    upper_inner = -ratio * take_rows(conduct, 1, count, axis_index)
    diagonal = 1.0 - inner_lower - upper_inner
    positions = lax.broadcasted_iota(jnp.int32, inner_lower.shape, axis_index)
    first_lower = take_rows(inner_lower, 0, 1, axis_index)
    last_upper = take_rows(upper_inner, count - 2, count - 1, axis_index)
    solve_lower = jnp.where(positions == 0, 0.0, inner_lower)
    solve_upper = jnp.where(positions == count - 2, 0.0, upper_inner)
    from_prev = jnp.where(positions == 0, -first_lower, 0.0)
    from_next = jnp.where(positions == count - 2, -last_upper, 0.0)
    inner_rights = take_rows(rights, 0, count - 1, axis_index)
    local_part, prev_part, next_part = cyclic(
        solve_lower, diagonal, solve_upper, (inner_rights, from_prev, from_next), axis_index
    )
    tail_local = take_rows(local_part, count - 2, count - 1, axis_index)
    tail_prev = take_rows(prev_part, count - 2, count - 1, axis_index)
    tail_next = take_rows(next_part, count - 2, count - 1, axis_index)
    lower_last = take_rows(lower_band, count - 1, count, axis_index)
    right_last = take_rows(rights, count - 1, count, axis_index)
    head_coupling = take_rows(lower_band, 0, 1, axis_index)
    pieces = jnp.stack(
        [
            lower_last * tail_prev,
            1.0 - lower_last + lower_last * tail_next,
            right_last - lower_last * tail_local,
            head_coupling * (take_rows(prev_part, 0, 1, axis_index) - 1.0),
            head_coupling * take_rows(next_part, 0, 1, axis_index),
            head_coupling * take_rows(local_part, 0, 1, axis_index),
        ]
    )
    blocks = lax.axis_size(axis)
    copies = jnp.broadcast_to(pieces[None], (blocks,) + pieces.shape)
    previous, interface_value = reduced_solve(copies, ratio, axis)
    inner_values = local_part + prev_part * previous + next_part * interface_value
    return jnp.concatenate([inner_values, interface_value], axis=axis_index)


def on_device(thermal_state, sideways_face_flux_factor, downward_face_flux_factor):
    width = thermal_state.shape[2]
    count = lax.axis_size("lat")
    right_pairs = [(i, i + 1) for i in range(count - 1)]
    left_pairs = [(i + 1, i) for i in range(count - 1)]
    first_cols = jnp.stack(
        [thermal_state[:, :, :1], sideways_face_flux_factor[:, :, :1]]
    )
    from_right = lax.ppermute(first_cols, "lat", left_pairs)
    from_left = lax.ppermute(thermal_state[:, :, width - 1 :], "lat", right_pairs)
    base, prev_weight, own_weight, pieces = depth_local(
        thermal_state,
        sideways_face_flux_factor,
        downward_face_flux_factor,
        from_right,
        from_left,
        lax.axis_size("depth"),
    )
    previous, interface_value = reduced_solve(pieces, ratio_z, "depth")
    reflected = base + prev_weight * previous + own_weight * interface_value
    return partition_solve(
        sideways_face_flux_factor, None, reflected, sideways_coupling_quotient, 2, "lat"
    )


def solution(mesh):
    in_specs = (P("depth", None, "lat"), P("depth", None, "lat"), P("depth", None, "lat"))
    out_specs = P("depth", None, "lat")
    return jax.shard_map(
        on_device, mesh=mesh, in_specs=in_specs, out_specs=out_specs, check_vma=False
    )
```

```python
import jax
import jax.numpy as jnp
from jax import lax
from jax.sharding import PartitionSpec as P
from jax.experimental import pallas as pl
from jax.experimental.pallas import tpu as pltpu

sideways_coupling_quotient = 20.0
ratio_z = 2000.0


def take_rows(values, start, stop, axis_index):
    return lax.slice_in_dim(values, start, stop, axis=axis_index)


def moved(values, stride, axis_index, filler, forward):
    count = values.shape[axis_index]
    pad_shape = list(values.shape)
    pad_shape[axis_index] = stride
    padding = jnp.full(pad_shape, filler, values.dtype)
    if forward:
        return jnp.concatenate(
            [take_rows(values, stride, count, axis_index), padding], axis=axis_index
        )
    return jnp.concatenate(
        [padding, take_rows(values, 0, count - stride, axis_index)], axis=axis_index
    )


def level_update(lower_band, diagonal, upper_band, rights, below, above):
    alpha_term = -lower_band / below[1]
    gamma_term = -upper_band / above[1]
    new_diagonal = diagonal + alpha_term * below[2] + gamma_term * above[0]
    new_rights = tuple(
        (
            column + alpha_term * low_col + gamma_term * high_col
            for column, low_col, high_col in zip(rights, below[3], above[3])
        )
    )
    return (alpha_term * below[0], new_diagonal, gamma_term * above[2], new_rights)


def cyclic(lower_band, diagonal, upper_band, rights, axis_index):
    count = lower_band.shape[axis_index]
    stride = 1
    while stride < count:
        below = (
            moved(lower_band, stride, axis_index, 0.0, False),
            moved(diagonal, stride, axis_index, 1.0, False),
            moved(upper_band, stride, axis_index, 0.0, False),
            tuple((moved(column, stride, axis_index, 0.0, False) for column in rights)),
        )
        above = (
            moved(lower_band, stride, axis_index, 0.0, True),
            moved(diagonal, stride, axis_index, 1.0, True),
            moved(upper_band, stride, axis_index, 0.0, True),
            tuple((moved(column, stride, axis_index, 0.0, True) for column in rights)),
        )
        lower_band, diagonal, upper_band, rights = level_update(
            lower_band, diagonal, upper_band, rights, below, above
        )
        stride = stride * 2
    return tuple((column / diagonal for column in rights))


def depth_kernel(t_ref, s_ref, d_ref, right_ref, tl_ref, base_ref, p_ref, n_ref, pieces_ref):
    rows, _, width = t_ref.shape
    temp = t_ref[...]
    conduct = s_ref[...]
    lane = lax.broadcasted_iota(jnp.int32, temp.shape, 2)
    last = lane == width - 1
    first = lane == 0
    temp_right = jnp.where(last, right_ref[0], pltpu.roll(temp, width - 1, 2))
    conduct_right = jnp.where(last, right_ref[1], pltpu.roll(conduct, width - 1, 2))
    temp_left = jnp.where(first, tl_ref[...], pltpu.roll(temp, 1, 2))
    base_ref[...] = temp + sideways_coupling_quotient * (
        conduct_right * (temp_right - temp) - conduct * (temp - temp_left)
    )
    inner = rows - 1
    lower = [-ratio_z * d_ref[i] for i in range(rows)]
    upper = [lower[i + 1] for i in range(inner)]
    c_term, r_local, r_prev = [], [], []
    r_next = None
    for i in range(inner):
        diagonal = 1.0 - lower[i] - upper[i]
        rhs = base_ref[i]
        if i == 0:
            den = diagonal
            local = rhs / den
            prev = -lower[i] / den
        else:
            den = diagonal - lower[i] * c_term[i - 1]
            local = (rhs - lower[i] * r_local[i - 1]) / den
            prev = (-lower[i] * r_prev[i - 1]) / den
        if i < inner - 1:
            c_term.append(upper[i] / den)
        else:
            c_term.append(None)
            r_next = -upper[i] / den
        r_local.append(local)
        r_prev.append(prev)
    local = r_local[inner - 1]
    prev = r_prev[inner - 1]
    nxt = r_next
    lower_last = lower[rows - 1]
    right_last = base_ref[rows - 1]
    own_lower = lower_last * prev
    own_diag = 1.0 - lower_last + lower_last * nxt
    own_right = right_last - lower_last * local
    base_ref[rows - 1] = -right_last
    p_ref[rows - 1] = jnp.zeros_like(local)
    n_ref[rows - 1] = jnp.full_like(local, 2.0)
    for i in range(inner - 1, -1, -1):
        if i < inner - 1:
            local = r_local[i] - c_term[i] * local
            prev = r_prev[i] - c_term[i] * prev
            nxt = -c_term[i] * nxt
        base_ref[i] = 2.0 * local - base_ref[i]
        p_ref[i] = 2.0 * prev
        n_ref[i] = 2.0 * nxt
    head_coupling = lower[0]
    own = (
        own_lower,
        own_diag,
        own_right,
        head_coupling * (prev - 1.0),
        head_coupling * nxt,
        head_coupling * local,
    )
    for block in range(pieces_ref.shape[0]):
        for i in range(6):
            pieces_ref[block, i] = own[i]


def depth_local(temp, conduct, downward, from_right, temp_prev, blocks):
    rows, lines, width = temp.shape
    full = jax.ShapeDtypeStruct(temp.shape, temp.dtype)
    copies = jax.ShapeDtypeStruct((blocks, 6, lines, width), temp.dtype)
    return pl.pallas_call(depth_kernel, out_shape=(full, full, full, copies))(
        temp, conduct, downward, from_right, temp_prev
    )


def lateral_kernel(base_ref, p_ref, n_ref, xp_ref, x_ref, s_ref, local_ref, prev_ref, next_ref, pieces_ref):
    rows, lines, width = s_ref.shape
    ratio = sideways_coupling_quotient
    rights = base_ref[...] + p_ref[...] * xp_ref[...][None] + n_ref[...] * x_ref[...][None]
    conduct = s_ref[...]
    lane = lax.broadcasted_iota(jnp.int32, conduct.shape, 2)
    inner = lane < width - 1
    conduct_next = pltpu.roll(conduct, width - 1, 2)
    lower_full = -ratio * conduct
    upper_full = -ratio * conduct_next
    diagonal = jnp.where(inner, 1.0 - lower_full - upper_full, 1.0)
    lower = jnp.where((lane >= 1) & inner, lower_full, 0.0)
    upper = jnp.where(lane < width - 2, upper_full, 0.0)
    columns = (
        jnp.where(inner, rights, 0.0),
        jnp.where(lane == 0, -lower_full, 0.0),
        jnp.where(lane == width - 2, -upper_full, 0.0),
    )
    stride = 1
    while stride < width:
        has_below = lane >= stride
        has_above = lane < width - stride

        def below(v, filler):
            return jnp.where(has_below, pltpu.roll(v, stride, 2), filler)

        def above(v, filler):
            return jnp.where(has_above, pltpu.roll(v, width - stride, 2), filler)

        alpha_term = -lower / below(diagonal, 1.0)
        gamma_term = -upper / above(diagonal, 1.0)
        new_diagonal = diagonal + alpha_term * below(upper, 0.0) + gamma_term * above(lower, 0.0)
        columns = tuple(
            column + alpha_term * below(column, 0.0) + gamma_term * above(column, 0.0)
            for column in columns
        )
        lower, upper = alpha_term * below(lower, 0.0), gamma_term * above(upper, 0.0)
        diagonal = new_diagonal
        stride = stride * 2
    local, prev, nxt = (column / diagonal for column in columns)
    local_ref[...] = local
    prev_ref[...] = prev
    next_ref[...] = nxt
    tail = [pltpu.roll(v, 1, 2) for v in (local, prev, nxt)]
    own_lower = lower_full * tail[1]
    own_diag = 1.0 - lower_full + lower_full * tail[2]
    own_right = rights - lower_full * tail[0]
    own = [v[:, :, width - 1 :] for v in (own_lower, own_diag, own_right)]
    heads = (lower_full * (prev - 1.0), lower_full * nxt, lower_full * local)
    own = own + [v[:, :, :1] for v in heads]
    for block in range(pieces_ref.shape[0]):
        for i in range(6):
            pieces_ref[block, i] = own[i]


def lateral_local(base, prev_weight, own_weight, previous, interface_value, conduct, blocks):
    rows, lines, width = conduct.shape
    full = jax.ShapeDtypeStruct(conduct.shape, conduct.dtype)
    copies = jax.ShapeDtypeStruct((blocks, 6, rows, lines, 1), conduct.dtype)
    return pl.pallas_call(lateral_kernel, out_shape=(full, full, full, copies))(
        base, prev_weight, own_weight, previous, interface_value, conduct
    )


def reduced_solve(copies, ratio, axis):
    line_shape = copies.shape[2:]
    every = lax.all_to_all(copies, axis, 0, 0, tiled=False)
    zero_row = jnp.zeros_like(every[:1, 0])
    from_next = [jnp.concatenate([every[1:, i], zero_row], axis=0) for i in (3, 4, 5)]
    red_diag = every[:, 1] + from_next[0]
    red_upper = from_next[1]
    red_right = every[:, 2] - from_next[2]
    solved = cyclic(every[:, 0], red_diag, red_upper, (red_right,), 0)[0]
    padded = jnp.concatenate([zero_row, solved], axis=0)
    index = lax.axis_index(axis)
    previous = lax.dynamic_slice_in_dim(padded, index, 1, 0)[0]
    interface_value = lax.dynamic_slice_in_dim(padded, index + 1, 1, 0)[0]
    return previous, interface_value


def partition_solve(conduct, first_next, rights, ratio, axis_index, axis):
    count = conduct.shape[axis_index]
    lower_band = -ratio * conduct
    inner_lower = take_rows(lower_band, 0, count - 1, axis_index)
    upper_inner = -ratio * take_rows(conduct, 1, count, axis_index)
    diagonal = 1.0 - inner_lower - upper_inner
    positions = lax.broadcasted_iota(jnp.int32, inner_lower.shape, axis_index)
    first_lower = take_rows(inner_lower, 0, 1, axis_index)
    last_upper = take_rows(upper_inner, count - 2, count - 1, axis_index)
    solve_lower = jnp.where(positions == 0, 0.0, inner_lower)
    solve_upper = jnp.where(positions == count - 2, 0.0, upper_inner)
    from_prev = jnp.where(positions == 0, -first_lower, 0.0)
    from_next = jnp.where(positions == count - 2, -last_upper, 0.0)
    inner_rights = take_rows(rights, 0, count - 1, axis_index)
    local_part, prev_part, next_part = cyclic(
        solve_lower, diagonal, solve_upper, (inner_rights, from_prev, from_next), axis_index
    )
    tail_local = take_rows(local_part, count - 2, count - 1, axis_index)
    tail_prev = take_rows(prev_part, count - 2, count - 1, axis_index)
    tail_next = take_rows(next_part, count - 2, count - 1, axis_index)
    lower_last = take_rows(lower_band, count - 1, count, axis_index)
    right_last = take_rows(rights, count - 1, count, axis_index)
    head_coupling = take_rows(lower_band, 0, 1, axis_index)
    pieces = jnp.stack(
        [
            lower_last * tail_prev,
            1.0 - lower_last + lower_last * tail_next,
            right_last - lower_last * tail_local,
            head_coupling * (take_rows(prev_part, 0, 1, axis_index) - 1.0),
            head_coupling * take_rows(next_part, 0, 1, axis_index),
            head_coupling * take_rows(local_part, 0, 1, axis_index),
        ]
    )
    blocks = lax.axis_size(axis)
    copies = jnp.broadcast_to(pieces[None], (blocks,) + pieces.shape)
    previous, interface_value = reduced_solve(copies, ratio, axis)
    inner_values = local_part + prev_part * previous + next_part * interface_value
    return jnp.concatenate([inner_values, interface_value], axis=axis_index)


def on_device(thermal_state, sideways_face_flux_factor, downward_face_flux_factor):
    width = thermal_state.shape[2]
    count = lax.axis_size("lat")
    right_pairs = [(i, i + 1) for i in range(count - 1)]
    left_pairs = [(i + 1, i) for i in range(count - 1)]
    first_cols = jnp.stack(
        [thermal_state[:, :, :1], sideways_face_flux_factor[:, :, :1]]
    )
    from_right = lax.ppermute(first_cols, "lat", left_pairs)
    from_left = lax.ppermute(thermal_state[:, :, width - 1 :], "lat", right_pairs)
    base, prev_weight, own_weight, pieces = depth_local(
        thermal_state,
        sideways_face_flux_factor,
        downward_face_flux_factor,
        from_right,
        from_left,
        lax.axis_size("depth"),
    )
    previous, interface_value = reduced_solve(pieces, ratio_z, "depth")
    local, prev, nxt, copies = lateral_local(
        base,
        prev_weight,
        own_weight,
        previous,
        interface_value,
        sideways_face_flux_factor,
        lax.axis_size("lat"),
    )
    previous, interface_value = reduced_solve(copies, sideways_coupling_quotient, "lat")
    lane = lax.broadcasted_iota(jnp.int32, local.shape, 2)
    return jnp.where(
        lane == width - 1, interface_value, local + prev * previous + nxt * interface_value
    )


def solution(mesh):
    in_specs = (P("depth", None, "lat"), P("depth", None, "lat"), P("depth", None, "lat"))
    out_specs = P("depth", None, "lat")
    return jax.shard_map(
        on_device, mesh=mesh, in_specs=in_specs, out_specs=out_specs, check_vma=False
    )
```

```python
import jax
import jax.numpy as jnp
from jax import lax
from jax.sharding import PartitionSpec as P
from jax.experimental import pallas as pl
from jax.experimental.pallas import tpu as pltpu

sideways_coupling_quotient = 20.0
ratio_z = 2000.0


def take_rows(values, start, stop, axis_index):
    return lax.slice_in_dim(values, start, stop, axis=axis_index)


def moved(values, stride, axis_index, filler, forward):
    count = values.shape[axis_index]
    pad_shape = list(values.shape)
    pad_shape[axis_index] = stride
    padding = jnp.full(pad_shape, filler, values.dtype)
    if forward:
        return jnp.concatenate(
            [take_rows(values, stride, count, axis_index), padding], axis=axis_index
        )
    return jnp.concatenate(
        [padding, take_rows(values, 0, count - stride, axis_index)], axis=axis_index
    )


def level_update(lower_band, diagonal, upper_band, rights, below, above):
    alpha_term = -lower_band / below[1]
    gamma_term = -upper_band / above[1]
    new_diagonal = diagonal + alpha_term * below[2] + gamma_term * above[0]
    new_rights = tuple(
        (
            column + alpha_term * low_col + gamma_term * high_col
            for column, low_col, high_col in zip(rights, below[3], above[3])
        )
    )
    return (alpha_term * below[0], new_diagonal, gamma_term * above[2], new_rights)


def cyclic_factors(lower_band, diagonal, upper_band, axis_index):
    count = lower_band.shape[axis_index]
    stride = 1
    levels = []
    while stride < count:
        alpha_term = -lower_band / moved(diagonal, stride, axis_index, 1.0, False)
        gamma_term = -upper_band / moved(diagonal, stride, axis_index, 1.0, True)
        new_diagonal = (
            diagonal
            + alpha_term * moved(upper_band, stride, axis_index, 0.0, False)
            + gamma_term * moved(lower_band, stride, axis_index, 0.0, True)
        )
        lower_band = alpha_term * moved(lower_band, stride, axis_index, 0.0, False)
        upper_band = gamma_term * moved(upper_band, stride, axis_index, 0.0, True)
        diagonal = new_diagonal
        levels.append((stride, alpha_term, gamma_term))
        stride = stride * 2
    return levels, diagonal


def cyclic_apply(factors, column, axis_index):
    levels, diagonal = factors
    for stride, alpha_term, gamma_term in levels:
        column = (
            column
            + alpha_term * moved(column, stride, axis_index, 0.0, False)
            + gamma_term * moved(column, stride, axis_index, 0.0, True)
        )
    return column / diagonal


def cyclic(lower_band, diagonal, upper_band, rights, axis_index):
    factors = cyclic_factors(lower_band, diagonal, upper_band, axis_index)
    return tuple(cyclic_apply(factors, column, axis_index) for column in rights)


def depth_kernel(t_ref, s_ref, d_ref, right_ref, tl_ref, base_ref, p_ref, n_ref, pieces_ref):
    rows, _, width = t_ref.shape
    temp = t_ref[...]
    conduct = s_ref[...]
    lane = lax.broadcasted_iota(jnp.int32, temp.shape, 2)
    last = lane == width - 1
    first = lane == 0
    temp_right = jnp.where(last, right_ref[0], pltpu.roll(temp, width - 1, 2))
    conduct_right = jnp.where(last, right_ref[1], pltpu.roll(conduct, width - 1, 2))
    temp_left = jnp.where(first, tl_ref[...], pltpu.roll(temp, 1, 2))
    base_ref[...] = temp + sideways_coupling_quotient * (
        conduct_right * (temp_right - temp) - conduct * (temp - temp_left)
    )
    inner = rows - 1
    lower = [-ratio_z * d_ref[i] for i in range(rows)]
    upper = [lower[i + 1] for i in range(inner)]
    c_term, r_local, r_prev = [], [], []
    r_next = None
    for i in range(inner):
        diagonal = 1.0 - lower[i] - upper[i]
        rhs = base_ref[i]
        if i == 0:
            den = diagonal
            local = rhs / den
            prev = -lower[i] / den
        else:
            den = diagonal - lower[i] * c_term[i - 1]
            local = (rhs - lower[i] * r_local[i - 1]) / den
            prev = (-lower[i] * r_prev[i - 1]) / den
        if i < inner - 1:
            c_term.append(upper[i] / den)
        else:
            c_term.append(None)
            r_next = -upper[i] / den
        r_local.append(local)
        r_prev.append(prev)
    local = r_local[inner - 1]
    prev = r_prev[inner - 1]
    nxt = r_next
    lower_last = lower[rows - 1]
    right_last = base_ref[rows - 1]
    own_lower = lower_last * prev
    own_diag = 1.0 - lower_last + lower_last * nxt
    own_right = right_last - lower_last * local
    base_ref[rows - 1] = -right_last
    p_ref[rows - 1] = jnp.zeros_like(local)
    n_ref[rows - 1] = jnp.full_like(local, 2.0)
    for i in range(inner - 1, -1, -1):
        if i < inner - 1:
            local = r_local[i] - c_term[i] * local
            prev = r_prev[i] - c_term[i] * prev
            nxt = -c_term[i] * nxt
        base_ref[i] = 2.0 * local - base_ref[i]
        p_ref[i] = 2.0 * prev
        n_ref[i] = 2.0 * nxt
    head_coupling = lower[0]
    own = (
        own_lower,
        own_diag,
        own_right,
        head_coupling * (prev - 1.0),
        head_coupling * nxt,
        head_coupling * local,
    )
    for block in range(pieces_ref.shape[0]):
        for i in range(6):
            pieces_ref[block, i] = own[i]


def depth_local(temp, conduct, downward, from_right, temp_prev, blocks):
    rows, lines, width = temp.shape
    full = jax.ShapeDtypeStruct(temp.shape, temp.dtype)
    copies = jax.ShapeDtypeStruct((blocks, 6, lines, width), temp.dtype)
    return pl.pallas_call(depth_kernel, out_shape=(full, full, full, copies))(
        temp, conduct, downward, from_right, temp_prev
    )


def reduced_solve(copies, ratio, axis):
    line_shape = copies.shape[2:]
    every = lax.all_to_all(copies, axis, 0, 0, tiled=False)
    zero_row = jnp.zeros_like(every[:1, 0])
    from_next = [jnp.concatenate([every[1:, i], zero_row], axis=0) for i in (3, 4, 5)]
    red_diag = every[:, 1] + from_next[0]
    red_upper = from_next[1]
    red_right = every[:, 2] - from_next[2]
    solved = cyclic(every[:, 0], red_diag, red_upper, (red_right,), 0)[0]
    padded = jnp.concatenate([zero_row, solved], axis=0)
    index = lax.axis_index(axis)
    previous = lax.dynamic_slice_in_dim(padded, index, 1, 0)[0]
    interface_value = lax.dynamic_slice_in_dim(padded, index + 1, 1, 0)[0]
    return previous, interface_value


def partition_solve(conduct, first_next, rights, ratio, axis_index, axis):
    count = conduct.shape[axis_index]
    lower_band = -ratio * conduct
    inner_lower = take_rows(lower_band, 0, count - 1, axis_index)
    upper_inner = -ratio * take_rows(conduct, 1, count, axis_index)
    diagonal = 1.0 - inner_lower - upper_inner
    positions = lax.broadcasted_iota(jnp.int32, inner_lower.shape, axis_index)
    first_lower = take_rows(inner_lower, 0, 1, axis_index)
    last_upper = take_rows(upper_inner, count - 2, count - 1, axis_index)
    solve_lower = jnp.where(positions == 0, 0.0, inner_lower)
    solve_upper = jnp.where(positions == count - 2, 0.0, upper_inner)
    from_prev = jnp.where(positions == 0, -first_lower, 0.0)
    from_next = jnp.where(positions == count - 2, -last_upper, 0.0)
    inner_rights = take_rows(rights, 0, count - 1, axis_index)
    factors = cyclic_factors(solve_lower, diagonal, solve_upper, axis_index)
    prev_part = cyclic_apply(factors, from_prev, axis_index)
    next_part = cyclic_apply(factors, from_next, axis_index)
    levels, last_diagonal = factors
    strides = [level[0] for level in levels]
    terms = [level[1:] for level in levels]
    terms, last_diagonal, prev_part, next_part = lax.optimization_barrier(
        (terms, last_diagonal, prev_part, next_part)
    )
    factors = ([(s,) + tuple(t) for s, t in zip(strides, terms)], last_diagonal)
    local_part = cyclic_apply(factors, inner_rights, axis_index)
    tail_local = take_rows(local_part, count - 2, count - 1, axis_index)
    tail_prev = take_rows(prev_part, count - 2, count - 1, axis_index)
    tail_next = take_rows(next_part, count - 2, count - 1, axis_index)
    lower_last = take_rows(lower_band, count - 1, count, axis_index)
    right_last = take_rows(rights, count - 1, count, axis_index)
    head_coupling = take_rows(lower_band, 0, 1, axis_index)
    pieces = jnp.stack(
        [
            lower_last * tail_prev,
            1.0 - lower_last + lower_last * tail_next,
            right_last - lower_last * tail_local,
            head_coupling * (take_rows(prev_part, 0, 1, axis_index) - 1.0),
            head_coupling * take_rows(next_part, 0, 1, axis_index),
            head_coupling * take_rows(local_part, 0, 1, axis_index),
        ]
    )
    blocks = lax.axis_size(axis)
    copies = jnp.broadcast_to(pieces[None], (blocks,) + pieces.shape)
    previous, interface_value = reduced_solve(copies, ratio, axis)
    inner_values = local_part + prev_part * previous + next_part * interface_value
    return jnp.concatenate([inner_values, interface_value], axis=axis_index)


def on_device(thermal_state, sideways_face_flux_factor, downward_face_flux_factor):
    width = thermal_state.shape[2]
    count = lax.axis_size("lat")
    right_pairs = [(i, i + 1) for i in range(count - 1)]
    left_pairs = [(i + 1, i) for i in range(count - 1)]
    first_cols = jnp.stack(
        [thermal_state[:, :, :1], sideways_face_flux_factor[:, :, :1]]
    )
    from_right = lax.ppermute(first_cols, "lat", left_pairs)
    from_left = lax.ppermute(thermal_state[:, :, width - 1 :], "lat", right_pairs)
    base, prev_weight, own_weight, pieces = depth_local(
        thermal_state,
        sideways_face_flux_factor,
        downward_face_flux_factor,
        from_right,
        from_left,
        lax.axis_size("depth"),
    )
    previous, interface_value = reduced_solve(pieces, ratio_z, "depth")
    reflected = base + prev_weight * previous + own_weight * interface_value
    return partition_solve(
        sideways_face_flux_factor, None, reflected, sideways_coupling_quotient, 2, "lat"
    )


def solution(mesh):
    in_specs = (P("depth", None, "lat"), P("depth", None, "lat"), P("depth", None, "lat"))
    out_specs = P("depth", None, "lat")
    return jax.shard_map(
        on_device, mesh=mesh, in_specs=in_specs, out_specs=out_specs, check_vma=False
    )
```

```python
import jax
import jax.numpy as jnp
from jax import lax
from jax.sharding import PartitionSpec as P
from jax.experimental import pallas as pl
from jax.experimental.pallas import tpu as pltpu

sideways_coupling_quotient = 20.0
ratio_z = 2000.0


def take_rows(values, start, stop, axis_index):
    return lax.slice_in_dim(values, start, stop, axis=axis_index)


def moved(values, stride, axis_index, filler, forward):
    count = values.shape[axis_index]
    pad_shape = list(values.shape)
    pad_shape[axis_index] = stride
    padding = jnp.full(pad_shape, filler, values.dtype)
    if forward:
        return jnp.concatenate(
            [take_rows(values, stride, count, axis_index), padding], axis=axis_index
        )
    return jnp.concatenate(
        [padding, take_rows(values, 0, count - stride, axis_index)], axis=axis_index
    )


def level_update(lower_band, diagonal, upper_band, rights, below, above):
    alpha_term = -lower_band / below[1]
    gamma_term = -upper_band / above[1]
    new_diagonal = diagonal + alpha_term * below[2] + gamma_term * above[0]
    new_rights = tuple(
        (
            column + alpha_term * low_col + gamma_term * high_col
            for column, low_col, high_col in zip(rights, below[3], above[3])
        )
    )
    return (alpha_term * below[0], new_diagonal, gamma_term * above[2], new_rights)


def cyclic_factors(lower_band, diagonal, upper_band, axis_index):
    count = lower_band.shape[axis_index]
    stride = 1
    levels = []
    while stride < count:
        alpha_term = -lower_band / moved(diagonal, stride, axis_index, 1.0, False)
        gamma_term = -upper_band / moved(diagonal, stride, axis_index, 1.0, True)
        new_diagonal = (
            diagonal
            + alpha_term * moved(upper_band, stride, axis_index, 0.0, False)
            + gamma_term * moved(lower_band, stride, axis_index, 0.0, True)
        )
        lower_band = alpha_term * moved(lower_band, stride, axis_index, 0.0, False)
        upper_band = gamma_term * moved(upper_band, stride, axis_index, 0.0, True)
        diagonal = new_diagonal
        levels.append((stride, alpha_term, gamma_term))
        stride = stride * 2
    return levels, diagonal


def cyclic_apply(factors, column, axis_index):
    levels, diagonal = factors
    for stride, alpha_term, gamma_term in levels:
        column = (
            column
            + alpha_term * moved(column, stride, axis_index, 0.0, False)
            + gamma_term * moved(column, stride, axis_index, 0.0, True)
        )
    return column / diagonal


def cyclic(lower_band, diagonal, upper_band, rights, axis_index):
    factors = cyclic_factors(lower_band, diagonal, upper_band, axis_index)
    return tuple(cyclic_apply(factors, column, axis_index) for column in rights)


def depth_kernel(t_ref, s_ref, d_ref, right_ref, tl_ref, base_ref, p_ref, n_ref, pieces_ref):
    rows, _, width = t_ref.shape
    temp = t_ref[...]
    conduct = s_ref[...]
    lane = lax.broadcasted_iota(jnp.int32, temp.shape, 2)
    last = lane == width - 1
    first = lane == 0
    temp_right = jnp.where(last, right_ref[0], pltpu.roll(temp, width - 1, 2))
    conduct_right = jnp.where(last, right_ref[1], pltpu.roll(conduct, width - 1, 2))
    temp_left = jnp.where(first, tl_ref[...], pltpu.roll(temp, 1, 2))
    base_ref[...] = temp + sideways_coupling_quotient * (
        conduct_right * (temp_right - temp) - conduct * (temp - temp_left)
    )
    inner = rows - 1
    lower = [-ratio_z * d_ref[i] for i in range(rows)]
    upper = [lower[i + 1] for i in range(inner)]
    c_term, r_local, r_prev = [], [], []
    r_next = None
    for i in range(inner):
        diagonal = 1.0 - lower[i] - upper[i]
        rhs = base_ref[i]
        if i == 0:
            den = diagonal
            local = rhs / den
            prev = -lower[i] / den
        else:
            den = diagonal - lower[i] * c_term[i - 1]
            local = (rhs - lower[i] * r_local[i - 1]) / den
            prev = (-lower[i] * r_prev[i - 1]) / den
        if i < inner - 1:
            c_term.append(upper[i] / den)
        else:
            c_term.append(None)
            r_next = -upper[i] / den
        r_local.append(local)
        r_prev.append(prev)
    local = r_local[inner - 1]
    prev = r_prev[inner - 1]
    nxt = r_next
    lower_last = lower[rows - 1]
    right_last = base_ref[rows - 1]
    own_lower = lower_last * prev
    own_diag = 1.0 - lower_last + lower_last * nxt
    own_right = right_last - lower_last * local
    base_ref[rows - 1] = -right_last
    p_ref[rows - 1] = jnp.zeros_like(local)
    n_ref[rows - 1] = jnp.full_like(local, 2.0)
    for i in range(inner - 1, -1, -1):
        if i < inner - 1:
            local = r_local[i] - c_term[i] * local
            prev = r_prev[i] - c_term[i] * prev
            nxt = -c_term[i] * nxt
        base_ref[i] = 2.0 * local - base_ref[i]
        p_ref[i] = 2.0 * prev
        n_ref[i] = 2.0 * nxt
    head_coupling = lower[0]
    own = (
        own_lower,
        own_diag,
        own_right,
        head_coupling * (prev - 1.0),
        head_coupling * nxt,
        head_coupling * local,
    )
    for block in range(pieces_ref.shape[0]):
        for i in range(6):
            pieces_ref[block, i] = own[i]


def depth_local(temp, conduct, downward, from_right, temp_prev, blocks):
    rows, lines, width = temp.shape
    full = jax.ShapeDtypeStruct(temp.shape, temp.dtype)
    copies = jax.ShapeDtypeStruct((blocks, 6, lines, width), temp.dtype)
    return pl.pallas_call(depth_kernel, out_shape=(full, full, full, copies))(
        temp, conduct, downward, from_right, temp_prev
    )


def reduced_solve(copies, ratio, axis):
    line_shape = copies.shape[2:]
    every = lax.all_to_all(copies, axis, 0, 0, tiled=False)
    zero_row = jnp.zeros_like(every[:1, 0])
    from_next = [jnp.concatenate([every[1:, i], zero_row], axis=0) for i in (3, 4, 5)]
    red_diag = every[:, 1] + from_next[0]
    red_upper = from_next[1]
    red_right = every[:, 2] - from_next[2]
    solved = cyclic(every[:, 0], red_diag, red_upper, (red_right,), 0)[0]
    padded = jnp.concatenate([zero_row, solved], axis=0)
    index = lax.axis_index(axis)
    previous = lax.dynamic_slice_in_dim(padded, index, 1, 0)[0]
    interface_value = lax.dynamic_slice_in_dim(padded, index + 1, 1, 0)[0]
    return previous, interface_value


def partition_solve(conduct, first_next, rights, ratio, axis_index, axis):
    count = conduct.shape[axis_index]
    lower_band = -ratio * conduct
    inner_lower = take_rows(lower_band, 0, count - 1, axis_index)
    upper_inner = -ratio * take_rows(conduct, 1, count, axis_index)
    diagonal = 1.0 - inner_lower - upper_inner
    positions = lax.broadcasted_iota(jnp.int32, inner_lower.shape, axis_index)
    first_lower = take_rows(inner_lower, 0, 1, axis_index)
    last_upper = take_rows(upper_inner, count - 2, count - 1, axis_index)
    solve_lower = jnp.where(positions == 0, 0.0, inner_lower)
    solve_upper = jnp.where(positions == count - 2, 0.0, upper_inner)
    from_prev = jnp.where(positions == 0, -first_lower, 0.0)
    from_next = jnp.where(positions == count - 2, -last_upper, 0.0)
    inner_rights = take_rows(rights, 0, count - 1, axis_index)
    factors = cyclic_factors(solve_lower, diagonal, solve_upper, axis_index)
    prev_part = cyclic_apply(factors, from_prev, axis_index)
    next_part = cyclic_apply(factors, from_next, axis_index)
    levels, last_diagonal = factors
    strides = [level[0] for level in levels]
    terms = [level[1:] for level in levels]
    terms, last_diagonal, prev_part, next_part = lax.optimization_barrier(
        (terms, last_diagonal, prev_part, next_part)
    )
    factors = ([(s,) + tuple(t) for s, t in zip(strides, terms)], last_diagonal)
    local_part = cyclic_apply(factors, inner_rights, axis_index)
    tail_local = take_rows(local_part, count - 2, count - 1, axis_index)
    tail_prev = take_rows(prev_part, count - 2, count - 1, axis_index)
    tail_next = take_rows(next_part, count - 2, count - 1, axis_index)
    lower_last = take_rows(lower_band, count - 1, count, axis_index)
    right_last = take_rows(rights, count - 1, count, axis_index)
    head_coupling = take_rows(lower_band, 0, 1, axis_index)
    pieces = jnp.stack(
        [
            lower_last * tail_prev,
            1.0 - lower_last + lower_last * tail_next,
            right_last - lower_last * tail_local,
            head_coupling * (take_rows(prev_part, 0, 1, axis_index) - 1.0),
            head_coupling * take_rows(next_part, 0, 1, axis_index),
            head_coupling * take_rows(local_part, 0, 1, axis_index),
        ]
    )
    blocks = lax.axis_size(axis)
    copies = jnp.broadcast_to(pieces[None], (blocks,) + pieces.shape)
    previous, interface_value = reduced_solve(copies, ratio, axis)
    inner_values = local_part + prev_part * previous + next_part * interface_value
    return jnp.concatenate([inner_values, interface_value], axis=axis_index)


def on_device(thermal_state, sideways_face_flux_factor, downward_face_flux_factor):
    width = thermal_state.shape[2]
    count = lax.axis_size("lat")
    right_pairs = [(i, i + 1) for i in range(count - 1)]
    left_pairs = [(i + 1, i) for i in range(count - 1)]
    first_cols = jnp.stack(
        [thermal_state[:, :, :1], sideways_face_flux_factor[:, :, :1]]
    )
    from_right = lax.ppermute(first_cols, "lat", left_pairs)
    from_left = lax.ppermute(thermal_state[:, :, width - 1 :], "lat", right_pairs)
    base, prev_weight, own_weight, pieces = depth_local(
        thermal_state,
        sideways_face_flux_factor,
        downward_face_flux_factor,
        from_right,
        from_left,
        lax.axis_size("depth"),
    )
    previous, interface_value = reduced_solve(pieces, ratio_z, "depth")
    lateral_conduct = lax.optimization_barrier((sideways_face_flux_factor, pieces))[0]
    reflected = base + prev_weight * previous + own_weight * interface_value
    return partition_solve(
        lateral_conduct, None, reflected, sideways_coupling_quotient, 2, "lat"
    )


def solution(mesh):
    in_specs = (P("depth", None, "lat"), P("depth", None, "lat"), P("depth", None, "lat"))
    out_specs = P("depth", None, "lat")
    return jax.shard_map(
        on_device, mesh=mesh, in_specs=in_specs, out_specs=out_specs, check_vma=False
    )
```

```python
import jax
import jax.numpy as jnp
from jax import lax
from jax.sharding import PartitionSpec as P
from jax.experimental import pallas as pl
from jax.experimental.pallas import tpu as pltpu

sideways_coupling_quotient = 20.0
ratio_z = 2000.0


def take_rows(values, start, stop, axis_index):
    return lax.slice_in_dim(values, start, stop, axis=axis_index)


def moved(values, stride, axis_index, filler, forward):
    count = values.shape[axis_index]
    pad_shape = list(values.shape)
    pad_shape[axis_index] = stride
    padding = jnp.full(pad_shape, filler, values.dtype)
    if forward:
        return jnp.concatenate(
            [take_rows(values, stride, count, axis_index), padding], axis=axis_index
        )
    return jnp.concatenate(
        [padding, take_rows(values, 0, count - stride, axis_index)], axis=axis_index
    )


def level_update(lower_band, diagonal, upper_band, rights, below, above):
    alpha_term = -lower_band / below[1]
    gamma_term = -upper_band / above[1]
    new_diagonal = diagonal + alpha_term * below[2] + gamma_term * above[0]
    new_rights = tuple(
        (
            column + alpha_term * low_col + gamma_term * high_col
            for column, low_col, high_col in zip(rights, below[3], above[3])
        )
    )
    return (alpha_term * below[0], new_diagonal, gamma_term * above[2], new_rights)


def cyclic_factors(lower_band, diagonal, upper_band, axis_index):
    count = lower_band.shape[axis_index]
    stride = 1
    levels = []
    while stride < count:
        alpha_term = -lower_band / moved(diagonal, stride, axis_index, 1.0, False)
        gamma_term = -upper_band / moved(diagonal, stride, axis_index, 1.0, True)
        new_diagonal = (
            diagonal
            + alpha_term * moved(upper_band, stride, axis_index, 0.0, False)
            + gamma_term * moved(lower_band, stride, axis_index, 0.0, True)
        )
        lower_band = alpha_term * moved(lower_band, stride, axis_index, 0.0, False)
        upper_band = gamma_term * moved(upper_band, stride, axis_index, 0.0, True)
        diagonal = new_diagonal
        levels.append((stride, alpha_term, gamma_term))
        stride = stride * 2
    return levels, diagonal


def cyclic_apply(factors, column, axis_index):
    levels, diagonal = factors
    for stride, alpha_term, gamma_term in levels:
        column = (
            column
            + alpha_term * moved(column, stride, axis_index, 0.0, False)
            + gamma_term * moved(column, stride, axis_index, 0.0, True)
        )
    return column / diagonal


def cyclic(lower_band, diagonal, upper_band, rights, axis_index):
    factors = cyclic_factors(lower_band, diagonal, upper_band, axis_index)
    return tuple(cyclic_apply(factors, column, axis_index) for column in rights)


def depth_kernel(t_ref, s_ref, d_ref, right_ref, tl_ref, base_ref, p_ref, n_ref, pieces_ref):
    rows, _, width = t_ref.shape
    temp = t_ref[...]
    conduct = s_ref[...]
    lane = lax.broadcasted_iota(jnp.int32, temp.shape, 2)
    last = lane == width - 1
    first = lane == 0
    temp_right = jnp.where(last, right_ref[0], pltpu.roll(temp, width - 1, 2))
    conduct_right = jnp.where(last, right_ref[1], pltpu.roll(conduct, width - 1, 2))
    temp_left = jnp.where(first, tl_ref[...], pltpu.roll(temp, 1, 2))
    base_ref[...] = temp + sideways_coupling_quotient * (
        conduct_right * (temp_right - temp) - conduct * (temp - temp_left)
    )
    inner = rows - 1
    lower = [-ratio_z * d_ref[i] for i in range(rows)]
    upper = [lower[i + 1] for i in range(inner)]
    c_term, r_local, r_prev = [], [], []
    r_next = None
    for i in range(inner):
        diagonal = 1.0 - lower[i] - upper[i]
        rhs = base_ref[i]
        if i == 0:
            den = diagonal
            local = rhs / den
            prev = -lower[i] / den
        else:
            den = diagonal - lower[i] * c_term[i - 1]
            local = (rhs - lower[i] * r_local[i - 1]) / den
            prev = (-lower[i] * r_prev[i - 1]) / den
        if i < inner - 1:
            c_term.append(upper[i] / den)
        else:
            c_term.append(None)
            r_next = -upper[i] / den
        r_local.append(local)
        r_prev.append(prev)
    local = r_local[inner - 1]
    prev = r_prev[inner - 1]
    nxt = r_next
    lower_last = lower[rows - 1]
    right_last = base_ref[rows - 1]
    own_lower = lower_last * prev
    own_diag = 1.0 - lower_last + lower_last * nxt
    own_right = right_last - lower_last * local
    base_ref[rows - 1] = -right_last
    p_ref[rows - 1] = jnp.zeros_like(local)
    n_ref[rows - 1] = jnp.full_like(local, 2.0)
    for i in range(inner - 1, -1, -1):
        if i < inner - 1:
            local = r_local[i] - c_term[i] * local
            prev = r_prev[i] - c_term[i] * prev
            nxt = -c_term[i] * nxt
        base_ref[i] = 2.0 * local - base_ref[i]
        p_ref[i] = 2.0 * prev
        n_ref[i] = 2.0 * nxt
    head_coupling = lower[0]
    own = (
        own_lower,
        own_diag,
        own_right,
        head_coupling * (prev - 1.0),
        head_coupling * nxt,
        head_coupling * local,
    )
    for block in range(pieces_ref.shape[0]):
        for i in range(6):
            pieces_ref[block, i] = own[i]


def depth_local(temp, conduct, downward, from_right, temp_prev, blocks):
    rows, lines, width = temp.shape
    full = jax.ShapeDtypeStruct(temp.shape, temp.dtype)
    copies = jax.ShapeDtypeStruct((blocks, 6, lines, width), temp.dtype)
    return pl.pallas_call(depth_kernel, out_shape=(full, full, full, copies))(
        temp, conduct, downward, from_right, temp_prev
    )


def reduced_solve(copies, ratio, axis):
    line_shape = copies.shape[2:]
    every = lax.all_to_all(copies, axis, 0, 0, tiled=False)
    zero_row = jnp.zeros_like(every[:1, 0])
    from_next = [jnp.concatenate([every[1:, i], zero_row], axis=0) for i in (3, 4, 5)]
    red_diag = every[:, 1] + from_next[0]
    red_upper = from_next[1]
    red_right = every[:, 2] - from_next[2]
    solved = cyclic(every[:, 0], red_diag, red_upper, (red_right,), 0)[0]
    padded = jnp.concatenate([zero_row, solved], axis=0)
    index = lax.axis_index(axis)
    previous = lax.dynamic_slice_in_dim(padded, index, 1, 0)[0]
    interface_value = lax.dynamic_slice_in_dim(padded, index + 1, 1, 0)[0]
    return previous, interface_value


def partition_solve(conduct, first_next, rights, ratio, axis_index, axis):
    count = conduct.shape[axis_index]
    lower_band = -ratio * conduct
    inner_lower = take_rows(lower_band, 0, count - 1, axis_index)
    upper_inner = -ratio * take_rows(conduct, 1, count, axis_index)
    diagonal = 1.0 - inner_lower - upper_inner
    positions = lax.broadcasted_iota(jnp.int32, inner_lower.shape, axis_index)
    first_lower = take_rows(inner_lower, 0, 1, axis_index)
    last_upper = take_rows(upper_inner, count - 2, count - 1, axis_index)
    solve_lower = jnp.where(positions == 0, 0.0, inner_lower)
    solve_upper = jnp.where(positions == count - 2, 0.0, upper_inner)
    from_prev = jnp.where(positions == 0, -first_lower, 0.0)
    from_next = jnp.where(positions == count - 2, -last_upper, 0.0)
    inner_rights = take_rows(rights, 0, count - 1, axis_index)
    factors = cyclic_factors(solve_lower, diagonal, solve_upper, axis_index)
    prev_part = cyclic_apply(factors, from_prev, axis_index)
    next_part = cyclic_apply(factors, from_next, axis_index)
    levels, last_diagonal = factors
    strides = [level[0] for level in levels]
    terms = [level[1:] for level in levels]
    terms, last_diagonal, prev_part, next_part = lax.optimization_barrier(
        (terms, last_diagonal, prev_part, next_part)
    )
    factors = ([(s,) + tuple(t) for s, t in zip(strides, terms)], last_diagonal)
    local_part = cyclic_apply(factors, inner_rights, axis_index)
    tail_local = take_rows(local_part, count - 2, count - 1, axis_index)
    tail_prev = take_rows(prev_part, count - 2, count - 1, axis_index)
    tail_next = take_rows(next_part, count - 2, count - 1, axis_index)
    lower_last = take_rows(lower_band, count - 1, count, axis_index)
    right_last = take_rows(rights, count - 1, count, axis_index)
    head_coupling = take_rows(lower_band, 0, 1, axis_index)
    pieces = jnp.stack(
        [
            lower_last * tail_prev,
            1.0 - lower_last + lower_last * tail_next,
            right_last - lower_last * tail_local,
            head_coupling * (take_rows(prev_part, 0, 1, axis_index) - 1.0),
            head_coupling * take_rows(next_part, 0, 1, axis_index),
            head_coupling * take_rows(local_part, 0, 1, axis_index),
        ]
    )
    blocks = lax.axis_size(axis)
    flat = pieces.reshape(pieces.shape[0], -1)
    copies = jnp.broadcast_to(flat[None], (blocks,) + flat.shape)
    previous, interface_value = reduced_solve(copies, ratio, axis)
    previous = previous.reshape(pieces.shape[1:])
    interface_value = interface_value.reshape(pieces.shape[1:])
    inner_values = local_part + prev_part * previous + next_part * interface_value
    return jnp.concatenate([inner_values, interface_value], axis=axis_index)


def on_device(thermal_state, sideways_face_flux_factor, downward_face_flux_factor):
    width = thermal_state.shape[2]
    count = lax.axis_size("lat")
    right_pairs = [(i, i + 1) for i in range(count - 1)]
    left_pairs = [(i + 1, i) for i in range(count - 1)]
    first_cols = jnp.stack(
        [thermal_state[:, :, :1], sideways_face_flux_factor[:, :, :1]]
    )
    from_right = lax.ppermute(first_cols, "lat", left_pairs)
    from_left = lax.ppermute(thermal_state[:, :, width - 1 :], "lat", right_pairs)
    base, prev_weight, own_weight, pieces = depth_local(
        thermal_state,
        sideways_face_flux_factor,
        downward_face_flux_factor,
        from_right,
        from_left,
        lax.axis_size("depth"),
    )
    previous, interface_value = reduced_solve(pieces, ratio_z, "depth")
    lateral_conduct = lax.optimization_barrier((sideways_face_flux_factor, pieces))[0]
    reflected = base + prev_weight * previous + own_weight * interface_value
    return partition_solve(
        lateral_conduct, None, reflected, sideways_coupling_quotient, 2, "lat"
    )


def solution(mesh):
    in_specs = (P("depth", None, "lat"), P("depth", None, "lat"), P("depth", None, "lat"))
    out_specs = P("depth", None, "lat")
    return jax.shard_map(
        on_device, mesh=mesh, in_specs=in_specs, out_specs=out_specs, check_vma=False
    )
```

```python
import jax
import jax.numpy as jnp
from jax import lax
from jax.sharding import PartitionSpec as P
from jax.experimental import pallas as pl
from jax.experimental.pallas import tpu as pltpu

sideways_coupling_quotient = 20.0
ratio_z = 2000.0


def take_rows(values, start, stop, axis_index):
    return lax.slice_in_dim(values, start, stop, axis=axis_index)


def moved(values, stride, axis_index, filler, forward):
    count = values.shape[axis_index]
    pad_shape = list(values.shape)
    pad_shape[axis_index] = stride
    padding = jnp.full(pad_shape, filler, values.dtype)
    if forward:
        return jnp.concatenate(
            [take_rows(values, stride, count, axis_index), padding], axis=axis_index
        )
    return jnp.concatenate(
        [padding, take_rows(values, 0, count - stride, axis_index)], axis=axis_index
    )


def level_update(lower_band, diagonal, upper_band, rights, below, above):
    alpha_term = -lower_band / below[1]
    gamma_term = -upper_band / above[1]
    new_diagonal = diagonal + alpha_term * below[2] + gamma_term * above[0]
    new_rights = tuple(
        (
            column + alpha_term * low_col + gamma_term * high_col
            for column, low_col, high_col in zip(rights, below[3], above[3])
        )
    )
    return (alpha_term * below[0], new_diagonal, gamma_term * above[2], new_rights)


def cyclic_factors(lower_band, diagonal, upper_band, axis_index):
    count = lower_band.shape[axis_index]
    stride = 1
    levels = []
    while stride < count:
        alpha_term = -lower_band / moved(diagonal, stride, axis_index, 1.0, False)
        gamma_term = -upper_band / moved(diagonal, stride, axis_index, 1.0, True)
        new_diagonal = (
            diagonal
            + alpha_term * moved(upper_band, stride, axis_index, 0.0, False)
            + gamma_term * moved(lower_band, stride, axis_index, 0.0, True)
        )
        lower_band = alpha_term * moved(lower_band, stride, axis_index, 0.0, False)
        upper_band = gamma_term * moved(upper_band, stride, axis_index, 0.0, True)
        diagonal = new_diagonal
        levels.append((stride, alpha_term, gamma_term))
        stride = stride * 2
    return levels, diagonal


def cyclic_apply(factors, column, axis_index):
    levels, diagonal = factors
    for stride, alpha_term, gamma_term in levels:
        column = (
            column
            + alpha_term * moved(column, stride, axis_index, 0.0, False)
            + gamma_term * moved(column, stride, axis_index, 0.0, True)
        )
    return column / diagonal


def cyclic(lower_band, diagonal, upper_band, rights, axis_index):
    factors = cyclic_factors(lower_band, diagonal, upper_band, axis_index)
    return tuple(cyclic_apply(factors, column, axis_index) for column in rights)


def depth_factor_kernel(d_ref, den_ref, c_ref, p_ref, n_ref, fixed_ref):
    rows = d_ref.shape[0]
    inner = rows - 1
    lower = [-ratio_z * d_ref[i] for i in range(rows)]
    upper = [lower[i + 1] for i in range(inner)]
    c_term, r_prev = [], []
    r_next = None
    for i in range(inner):
        diagonal = 1.0 - lower[i] - upper[i]
        if i == 0:
            den = diagonal
            prev = -lower[i] / den
        else:
            den = diagonal - lower[i] * c_term[i - 1]
            prev = (-lower[i] * r_prev[i - 1]) / den
        den_ref[i] = den
        if i < inner - 1:
            c_term.append(upper[i] / den)
            c_ref[i] = c_term[i]
        else:
            c_term.append(None)
            r_next = -upper[i] / den
        r_prev.append(prev)
    prev = r_prev[inner - 1]
    nxt = r_next
    lower_last = lower[rows - 1]
    fixed_ref[0] = lower_last * prev
    fixed_ref[1] = 1.0 - lower_last + lower_last * nxt
    p_ref[rows - 1] = jnp.zeros_like(prev)
    n_ref[rows - 1] = jnp.full_like(prev, 2.0)
    for i in range(inner - 1, -1, -1):
        if i < inner - 1:
            prev = r_prev[i] - c_term[i] * prev
            nxt = -c_term[i] * nxt
        p_ref[i] = 2.0 * prev
        n_ref[i] = 2.0 * nxt
    fixed_ref[2] = lower[0] * (prev - 1.0)
    fixed_ref[3] = lower[0] * nxt


def depth_kernel(t_ref, s_ref, d_ref, right_ref, tl_ref, den_ref, c_ref, fixed_ref, base_ref, pieces_ref):
    rows, _, width = t_ref.shape
    temp = t_ref[...]
    conduct = s_ref[...]
    lane = lax.broadcasted_iota(jnp.int32, temp.shape, 2)
    last = lane == width - 1
    first = lane == 0
    temp_right = jnp.where(last, right_ref[0], pltpu.roll(temp, width - 1, 2))
    conduct_right = jnp.where(last, right_ref[1], pltpu.roll(conduct, width - 1, 2))
    temp_left = jnp.where(first, tl_ref[...], pltpu.roll(temp, 1, 2))
    base_ref[...] = temp + sideways_coupling_quotient * (
        conduct_right * (temp_right - temp) - conduct * (temp - temp_left)
    )
    inner = rows - 1
    r_local = []
    for i in range(inner):
        rhs = base_ref[i]
        if i == 0:
            local = rhs / den_ref[i]
        else:
            local = (rhs - (-ratio_z * d_ref[i]) * r_local[i - 1]) / den_ref[i]
        r_local.append(local)
    local = r_local[inner - 1]
    lower_last = -ratio_z * d_ref[rows - 1]
    right_last = base_ref[rows - 1]
    own_right = right_last - lower_last * local
    base_ref[rows - 1] = -right_last
    for i in range(inner - 1, -1, -1):
        if i < inner - 1:
            local = r_local[i] - c_ref[i] * local
        base_ref[i] = 2.0 * local - base_ref[i]
    own = (
        fixed_ref[0],
        fixed_ref[1],
        own_right,
        fixed_ref[2],
        fixed_ref[3],
        (-ratio_z * d_ref[0]) * local,
    )
    for block in range(pieces_ref.shape[0]):
        for i in range(6):
            pieces_ref[block, i] = own[i]


def depth_local(temp, conduct, downward, from_right, temp_prev, blocks):
    rows, lines, width = temp.shape
    full = jax.ShapeDtypeStruct(temp.shape, temp.dtype)
    inner = jax.ShapeDtypeStruct((rows - 1, lines, width), temp.dtype)
    den, c_term, prev_weight, own_weight, fixed = pl.pallas_call(
        depth_factor_kernel,
        out_shape=(inner, inner, full, full, jax.ShapeDtypeStruct((4, lines, width), temp.dtype)),
    )(downward)
    copies = jax.ShapeDtypeStruct((blocks, 6, lines, width), temp.dtype)
    base, pieces = pl.pallas_call(depth_kernel, out_shape=(full, copies))(
        temp, conduct, downward, from_right, temp_prev, den, c_term, fixed
    )
    return base, prev_weight, own_weight, pieces


def reduced_solve(copies, ratio, axis):
    line_shape = copies.shape[2:]
    every = lax.all_to_all(copies, axis, 0, 0, tiled=False)
    zero_row = jnp.zeros_like(every[:1, 0])
    from_next = [jnp.concatenate([every[1:, i], zero_row], axis=0) for i in (3, 4, 5)]
    red_diag = every[:, 1] + from_next[0]
    red_upper = from_next[1]
    red_right = every[:, 2] - from_next[2]
    solved = cyclic(every[:, 0], red_diag, red_upper, (red_right,), 0)[0]
    padded = jnp.concatenate([zero_row, solved], axis=0)
    index = lax.axis_index(axis)
    previous = lax.dynamic_slice_in_dim(padded, index, 1, 0)[0]
    interface_value = lax.dynamic_slice_in_dim(padded, index + 1, 1, 0)[0]
    return previous, interface_value


def partition_solve(conduct, first_next, rights, ratio, axis_index, axis):
    count = conduct.shape[axis_index]
    lower_band = -ratio * conduct
    inner_lower = take_rows(lower_band, 0, count - 1, axis_index)
    upper_inner = -ratio * take_rows(conduct, 1, count, axis_index)
    diagonal = 1.0 - inner_lower - upper_inner
    positions = lax.broadcasted_iota(jnp.int32, inner_lower.shape, axis_index)
    first_lower = take_rows(inner_lower, 0, 1, axis_index)
    last_upper = take_rows(upper_inner, count - 2, count - 1, axis_index)
    solve_lower = jnp.where(positions == 0, 0.0, inner_lower)
    solve_upper = jnp.where(positions == count - 2, 0.0, upper_inner)
    from_prev = jnp.where(positions == 0, -first_lower, 0.0)
    from_next = jnp.where(positions == count - 2, -last_upper, 0.0)
    inner_rights = take_rows(rights, 0, count - 1, axis_index)
    factors = cyclic_factors(solve_lower, diagonal, solve_upper, axis_index)
    prev_part = cyclic_apply(factors, from_prev, axis_index)
    next_part = cyclic_apply(factors, from_next, axis_index)
    levels, last_diagonal = factors
    strides = [level[0] for level in levels]
    terms = [level[1:] for level in levels]
    terms, last_diagonal, prev_part, next_part = lax.optimization_barrier(
        (terms, last_diagonal, prev_part, next_part)
    )
    factors = ([(s,) + tuple(t) for s, t in zip(strides, terms)], last_diagonal)
    local_part = cyclic_apply(factors, inner_rights, axis_index)
    tail_local = take_rows(local_part, count - 2, count - 1, axis_index)
    tail_prev = take_rows(prev_part, count - 2, count - 1, axis_index)
    tail_next = take_rows(next_part, count - 2, count - 1, axis_index)
    lower_last = take_rows(lower_band, count - 1, count, axis_index)
    right_last = take_rows(rights, count - 1, count, axis_index)
    head_coupling = take_rows(lower_band, 0, 1, axis_index)
    pieces = jnp.stack(
        [
            lower_last * tail_prev,
            1.0 - lower_last + lower_last * tail_next,
            right_last - lower_last * tail_local,
            head_coupling * (take_rows(prev_part, 0, 1, axis_index) - 1.0),
            head_coupling * take_rows(next_part, 0, 1, axis_index),
            head_coupling * take_rows(local_part, 0, 1, axis_index),
        ]
    )
    blocks = lax.axis_size(axis)
    flat = pieces.reshape(pieces.shape[0], -1)
    copies = jnp.broadcast_to(flat[None], (blocks,) + flat.shape)
    previous, interface_value = reduced_solve(copies, ratio, axis)
    previous = previous.reshape(pieces.shape[1:])
    interface_value = interface_value.reshape(pieces.shape[1:])
    inner_values = local_part + prev_part * previous + next_part * interface_value
    return jnp.concatenate([inner_values, interface_value], axis=axis_index)


def on_device(thermal_state, sideways_face_flux_factor, downward_face_flux_factor):
    width = thermal_state.shape[2]
    count = lax.axis_size("lat")
    right_pairs = [(i, i + 1) for i in range(count - 1)]
    left_pairs = [(i + 1, i) for i in range(count - 1)]
    first_cols = jnp.stack(
        [thermal_state[:, :, :1], sideways_face_flux_factor[:, :, :1]]
    )
    from_right = lax.ppermute(first_cols, "lat", left_pairs)
    from_left = lax.ppermute(thermal_state[:, :, width - 1 :], "lat", right_pairs)
    base, prev_weight, own_weight, pieces = depth_local(
        thermal_state,
        sideways_face_flux_factor,
        downward_face_flux_factor,
        from_right,
        from_left,
        lax.axis_size("depth"),
    )
    previous, interface_value = reduced_solve(pieces, ratio_z, "depth")
    lateral_conduct = lax.optimization_barrier((sideways_face_flux_factor, pieces))[0]
    reflected = base + prev_weight * previous + own_weight * interface_value
    return partition_solve(
        lateral_conduct, None, reflected, sideways_coupling_quotient, 2, "lat"
    )


def solution(mesh):
    in_specs = (P("depth", None, "lat"), P("depth", None, "lat"), P("depth", None, "lat"))
    out_specs = P("depth", None, "lat")
    return jax.shard_map(
        on_device, mesh=mesh, in_specs=in_specs, out_specs=out_specs, check_vma=False
    )
```

```python
import jax
import jax.numpy as jnp
from jax import lax
from jax.sharding import PartitionSpec as P
from jax.experimental import pallas as pl
from jax.experimental.pallas import tpu as pltpu

sideways_coupling_quotient = 20.0
ratio_z = 2000.0


def take_rows(values, start, stop, axis_index):
    return lax.slice_in_dim(values, start, stop, axis=axis_index)


def moved(values, stride, axis_index, filler, forward):
    count = values.shape[axis_index]
    pad_shape = list(values.shape)
    pad_shape[axis_index] = stride
    padding = jnp.full(pad_shape, filler, values.dtype)
    if forward:
        return jnp.concatenate(
            [take_rows(values, stride, count, axis_index), padding], axis=axis_index
        )
    return jnp.concatenate(
        [padding, take_rows(values, 0, count - stride, axis_index)], axis=axis_index
    )


def level_update(lower_band, diagonal, upper_band, rights, below, above):
    alpha_term = -lower_band / below[1]
    gamma_term = -upper_band / above[1]
    new_diagonal = diagonal + alpha_term * below[2] + gamma_term * above[0]
    new_rights = tuple(
        (
            column + alpha_term * low_col + gamma_term * high_col
            for column, low_col, high_col in zip(rights, below[3], above[3])
        )
    )
    return (alpha_term * below[0], new_diagonal, gamma_term * above[2], new_rights)


def cyclic_factors(lower_band, diagonal, upper_band, axis_index):
    count = lower_band.shape[axis_index]
    stride = 1
    levels = []
    while stride < count:
        alpha_term = -lower_band / moved(diagonal, stride, axis_index, 1.0, False)
        gamma_term = -upper_band / moved(diagonal, stride, axis_index, 1.0, True)
        new_diagonal = (
            diagonal
            + alpha_term * moved(upper_band, stride, axis_index, 0.0, False)
            + gamma_term * moved(lower_band, stride, axis_index, 0.0, True)
        )
        lower_band = alpha_term * moved(lower_band, stride, axis_index, 0.0, False)
        upper_band = gamma_term * moved(upper_band, stride, axis_index, 0.0, True)
        diagonal = new_diagonal
        levels.append((stride, alpha_term, gamma_term))
        stride = stride * 2
    return levels, diagonal


def cyclic_apply(factors, column, axis_index):
    levels, diagonal = factors
    for stride, alpha_term, gamma_term in levels:
        column = (
            column
            + alpha_term * moved(column, stride, axis_index, 0.0, False)
            + gamma_term * moved(column, stride, axis_index, 0.0, True)
        )
    return column / diagonal


def cyclic(lower_band, diagonal, upper_band, rights, axis_index):
    factors = cyclic_factors(lower_band, diagonal, upper_band, axis_index)
    return tuple(cyclic_apply(factors, column, axis_index) for column in rights)


def depth_factor_kernel(d_ref, den_ref, c_ref, p_ref, n_ref, fixed_ref):
    rows = d_ref.shape[0]
    inner = rows - 1
    lower = [-ratio_z * d_ref[i] for i in range(rows)]
    upper = [lower[i + 1] for i in range(inner)]
    c_term, r_prev = [], []
    r_next = None
    for i in range(inner):
        diagonal = 1.0 - lower[i] - upper[i]
        if i == 0:
            den = diagonal
            prev = -lower[i] / den
        else:
            den = diagonal - lower[i] * c_term[i - 1]
            prev = (-lower[i] * r_prev[i - 1]) / den
        den_ref[i] = den
        if i < inner - 1:
            c_term.append(upper[i] / den)
            c_ref[i] = c_term[i]
        else:
            c_term.append(None)
            r_next = -upper[i] / den
        r_prev.append(prev)
    prev = r_prev[inner - 1]
    nxt = r_next
    lower_last = lower[rows - 1]
    fixed_ref[0] = lower_last * prev
    fixed_ref[1] = 1.0 - lower_last + lower_last * nxt
    p_ref[rows - 1] = jnp.zeros_like(prev)
    n_ref[rows - 1] = jnp.full_like(prev, 2.0)
    for i in range(inner - 1, -1, -1):
        if i < inner - 1:
            prev = r_prev[i] - c_term[i] * prev
            nxt = -c_term[i] * nxt
        p_ref[i] = 2.0 * prev
        n_ref[i] = 2.0 * nxt
    fixed_ref[2] = lower[0] * (prev - 1.0)
    fixed_ref[3] = lower[0] * nxt


def depth_kernel(t_ref, s_ref, d_ref, right_ref, tl_ref, den_ref, c_ref, fixed_ref, base_ref, pieces_ref):
    rows, _, width = t_ref.shape
    temp = t_ref[...]
    conduct = s_ref[...]
    lane = lax.broadcasted_iota(jnp.int32, temp.shape, 2)
    last = lane == width - 1
    first = lane == 0
    temp_right = jnp.where(last, right_ref[0], pltpu.roll(temp, width - 1, 2))
    conduct_right = jnp.where(last, right_ref[1], pltpu.roll(conduct, width - 1, 2))
    temp_left = jnp.where(first, tl_ref[...], pltpu.roll(temp, 1, 2))
    base_ref[...] = temp + sideways_coupling_quotient * (
        conduct_right * (temp_right - temp) - conduct * (temp - temp_left)
    )
    inner = rows - 1
    r_local = []
    for i in range(inner):
        rhs = base_ref[i]
        if i == 0:
            local = rhs / den_ref[i]
        else:
            local = (rhs - (-ratio_z * d_ref[i]) * r_local[i - 1]) / den_ref[i]
        r_local.append(local)
    local = r_local[inner - 1]
    lower_last = -ratio_z * d_ref[rows - 1]
    right_last = base_ref[rows - 1]
    own_right = right_last - lower_last * local
    base_ref[rows - 1] = -right_last
    for i in range(inner - 1, -1, -1):
        if i < inner - 1:
            local = r_local[i] - c_ref[i] * local
        base_ref[i] = 2.0 * local - base_ref[i]
    own = (
        fixed_ref[0],
        fixed_ref[1],
        own_right,
        fixed_ref[2],
        fixed_ref[3],
        (-ratio_z * d_ref[0]) * local,
    )
    for block in range(pieces_ref.shape[0]):
        for i in range(6):
            pieces_ref[block, i] = own[i]


def depth_local(temp, conduct, downward, from_right, temp_prev, blocks):
    rows, lines, width = temp.shape
    full = jax.ShapeDtypeStruct(temp.shape, temp.dtype)
    inner = jax.ShapeDtypeStruct((rows - 1, lines, width), temp.dtype)
    den, c_term, prev_weight, own_weight, fixed = pl.pallas_call(
        depth_factor_kernel,
        out_shape=(inner, inner, full, full, jax.ShapeDtypeStruct((4, lines, width), temp.dtype)),
    )(downward)
    copies = jax.ShapeDtypeStruct((blocks, 6, lines, width), temp.dtype)
    base, pieces = pl.pallas_call(depth_kernel, out_shape=(full, copies))(
        temp, conduct, downward, from_right, temp_prev, den, c_term, fixed
    )
    return base, prev_weight, own_weight, pieces


def reduced_solve(copies, ratio, axis):
    line_shape = copies.shape[2:]
    every = lax.all_to_all(copies, axis, 0, 0, tiled=False)
    zero_row = jnp.zeros_like(every[:1, 0])
    from_next = [jnp.concatenate([every[1:, i], zero_row], axis=0) for i in (3, 4, 5)]
    red_diag = every[:, 1] + from_next[0]
    red_upper = from_next[1]
    red_right = every[:, 2] - from_next[2]
    solved = cyclic(every[:, 0], red_diag, red_upper, (red_right,), 0)[0]
    padded = jnp.concatenate([zero_row, solved], axis=0)
    index = lax.axis_index(axis)
    previous = lax.dynamic_slice_in_dim(padded, index, 1, 0)[0]
    interface_value = lax.dynamic_slice_in_dim(padded, index + 1, 1, 0)[0]
    return previous, interface_value


def partition_solve(conduct, first_next, rights, ratio, axis_index, axis):
    count = conduct.shape[axis_index]
    lower_band = -ratio * conduct
    inner_lower = take_rows(lower_band, 0, count - 1, axis_index)
    upper_inner = -ratio * take_rows(conduct, 1, count, axis_index)
    diagonal = 1.0 - inner_lower - upper_inner
    positions = lax.broadcasted_iota(jnp.int32, inner_lower.shape, axis_index)
    first_lower = take_rows(inner_lower, 0, 1, axis_index)
    last_upper = take_rows(upper_inner, count - 2, count - 1, axis_index)
    solve_lower = jnp.where(positions == 0, 0.0, inner_lower)
    solve_upper = jnp.where(positions == count - 2, 0.0, upper_inner)
    from_prev = jnp.where(positions == 0, -first_lower, 0.0)
    from_next = jnp.where(positions == count - 2, -last_upper, 0.0)
    inner_rights = take_rows(rights, 0, count - 1, axis_index)
    factors = cyclic_factors(solve_lower, diagonal, solve_upper, axis_index)
    prev_part = cyclic_apply(factors, from_prev, axis_index)
    next_part = cyclic_apply(factors, from_next, axis_index)
    levels, last_diagonal = factors
    strides = [level[0] for level in levels]
    terms = [level[1:] for level in levels]
    terms, last_diagonal, prev_part, next_part = lax.optimization_barrier(
        (terms, last_diagonal, prev_part, next_part)
    )
    factors = ([(s,) + tuple(t) for s, t in zip(strides, terms)], last_diagonal)
    local_part = cyclic_apply(factors, inner_rights, axis_index)
    tail_local = take_rows(local_part, count - 2, count - 1, axis_index)
    tail_prev = take_rows(prev_part, count - 2, count - 1, axis_index)
    tail_next = take_rows(next_part, count - 2, count - 1, axis_index)
    lower_last = take_rows(lower_band, count - 1, count, axis_index)
    right_last = take_rows(rights, count - 1, count, axis_index)
    head_coupling = take_rows(lower_band, 0, 1, axis_index)
    pieces = jnp.stack(
        [
            lower_last * tail_prev,
            1.0 - lower_last + lower_last * tail_next,
            right_last - lower_last * tail_local,
            head_coupling * (take_rows(prev_part, 0, 1, axis_index) - 1.0),
            head_coupling * take_rows(next_part, 0, 1, axis_index),
            head_coupling * take_rows(local_part, 0, 1, axis_index),
        ]
    )
    blocks = lax.axis_size(axis)
    flat = pieces.reshape(pieces.shape[0], -1)
    copies = jnp.broadcast_to(flat[None], (blocks,) + flat.shape)
    previous, interface_value = reduced_solve(copies, ratio, axis)
    previous = previous.reshape(pieces.shape[1:])
    interface_value = interface_value.reshape(pieces.shape[1:])
    inner_values = local_part + prev_part * previous + next_part * interface_value
    return jnp.concatenate([inner_values, interface_value], axis=axis_index)


def on_device(thermal_state, sideways_face_flux_factor, downward_face_flux_factor):
    width = thermal_state.shape[2]
    count = lax.axis_size("lat")
    right_pairs = [(i, i + 1) for i in range(count - 1)]
    left_pairs = [(i + 1, i) for i in range(count - 1)]
    edge_shape = thermal_state.shape[:2] + (1,)
    first_cols = jnp.stack(
        [thermal_state[:, :, 0].reshape(-1), sideways_face_flux_factor[:, :, 0].reshape(-1)]
    )
    from_right = lax.ppermute(first_cols, "lat", left_pairs).reshape((2,) + edge_shape)
    last_col = thermal_state[:, :, width - 1].reshape(-1)
    from_left = lax.ppermute(last_col, "lat", right_pairs).reshape(edge_shape)
    base, prev_weight, own_weight, pieces = depth_local(
        thermal_state,
        sideways_face_flux_factor,
        downward_face_flux_factor,
        from_right,
        from_left,
        lax.axis_size("depth"),
    )
    previous, interface_value = reduced_solve(pieces, ratio_z, "depth")
    lateral_conduct = lax.optimization_barrier((sideways_face_flux_factor, pieces))[0]
    reflected = base + prev_weight * previous + own_weight * interface_value
    return partition_solve(
        lateral_conduct, None, reflected, sideways_coupling_quotient, 2, "lat"
    )


def solution(mesh):
    in_specs = (P("depth", None, "lat"), P("depth", None, "lat"), P("depth", None, "lat"))
    out_specs = P("depth", None, "lat")
    return jax.shard_map(
        on_device, mesh=mesh, in_specs=in_specs, out_specs=out_specs, check_vma=False
    )
```

```python
import jax
import jax.numpy as jnp
from jax import lax
from jax.sharding import PartitionSpec as P
from jax.experimental import pallas as pl
from jax.experimental.pallas import tpu as pltpu

sideways_coupling_quotient = 20.0
ratio_z = 2000.0


def take_rows(values, start, stop, axis_index):
    return lax.slice_in_dim(values, start, stop, axis=axis_index)


def moved(values, stride, axis_index, filler, forward):
    count = values.shape[axis_index]
    pad_shape = list(values.shape)
    pad_shape[axis_index] = stride
    padding = jnp.full(pad_shape, filler, values.dtype)
    if forward:
        return jnp.concatenate(
            [take_rows(values, stride, count, axis_index), padding], axis=axis_index
        )
    return jnp.concatenate(
        [padding, take_rows(values, 0, count - stride, axis_index)], axis=axis_index
    )


def level_update(lower_band, diagonal, upper_band, rights, below, above):
    alpha_term = -lower_band / below[1]
    gamma_term = -upper_band / above[1]
    new_diagonal = diagonal + alpha_term * below[2] + gamma_term * above[0]
    new_rights = tuple(
        (
            column + alpha_term * low_col + gamma_term * high_col
            for column, low_col, high_col in zip(rights, below[3], above[3])
        )
    )
    return (alpha_term * below[0], new_diagonal, gamma_term * above[2], new_rights)


def cyclic_factors(lower_band, diagonal, upper_band, axis_index):
    count = lower_band.shape[axis_index]
    stride = 1
    levels = []
    while stride < count:
        alpha_term = -lower_band / moved(diagonal, stride, axis_index, 1.0, False)
        gamma_term = -upper_band / moved(diagonal, stride, axis_index, 1.0, True)
        new_diagonal = (
            diagonal
            + alpha_term * moved(upper_band, stride, axis_index, 0.0, False)
            + gamma_term * moved(lower_band, stride, axis_index, 0.0, True)
        )
        lower_band = alpha_term * moved(lower_band, stride, axis_index, 0.0, False)
        upper_band = gamma_term * moved(upper_band, stride, axis_index, 0.0, True)
        diagonal = new_diagonal
        levels.append((stride, alpha_term, gamma_term))
        stride = stride * 2
    return levels, diagonal


def cyclic_apply(factors, column, axis_index):
    levels, diagonal = factors
    for stride, alpha_term, gamma_term in levels:
        column = (
            column
            + alpha_term * moved(column, stride, axis_index, 0.0, False)
            + gamma_term * moved(column, stride, axis_index, 0.0, True)
        )
    return column / diagonal


def cyclic(lower_band, diagonal, upper_band, rights, axis_index):
    factors = cyclic_factors(lower_band, diagonal, upper_band, axis_index)
    return tuple(cyclic_apply(factors, column, axis_index) for column in rights)


def depth_kernel(t_ref, s_ref, d_ref, right_ref, tl_ref, base_ref, p_ref, n_ref, pieces_ref):
    rows, _, width = t_ref.shape
    temp = t_ref[...]
    conduct = s_ref[...]
    lane = lax.broadcasted_iota(jnp.int32, temp.shape, 2)
    last = lane == width - 1
    first = lane == 0
    temp_right = jnp.where(last, right_ref[0], pltpu.roll(temp, width - 1, 2))
    conduct_right = jnp.where(last, right_ref[1], pltpu.roll(conduct, width - 1, 2))
    temp_left = jnp.where(first, tl_ref[...], pltpu.roll(temp, 1, 2))
    base_ref[...] = temp + sideways_coupling_quotient * (
        conduct_right * (temp_right - temp) - conduct * (temp - temp_left)
    )
    inner = rows - 1
    lower = [-ratio_z * d_ref[i] for i in range(rows)]
    upper = [lower[i + 1] for i in range(inner)]
    c_term, r_local, r_prev = [], [], []
    r_next = None
    for i in range(inner):
        diagonal = 1.0 - lower[i] - upper[i]
        rhs = base_ref[i]
        if i == 0:
            den = diagonal
            local = rhs / den
            prev = -lower[i] / den
        else:
            den = diagonal - lower[i] * c_term[i - 1]
            local = (rhs - lower[i] * r_local[i - 1]) / den
            prev = (-lower[i] * r_prev[i - 1]) / den
        if i < inner - 1:
            c_term.append(upper[i] / den)
        else:
            c_term.append(None)
            r_next = -upper[i] / den
        r_local.append(local)
        r_prev.append(prev)
    local = r_local[inner - 1]
    prev = r_prev[inner - 1]
    nxt = r_next
    lower_last = lower[rows - 1]
    right_last = base_ref[rows - 1]
    own_lower = lower_last * prev
    own_diag = 1.0 - lower_last + lower_last * nxt
    own_right = right_last - lower_last * local
    base_ref[rows - 1] = -right_last
    p_ref[rows - 1] = jnp.zeros_like(local)
    n_ref[rows - 1] = jnp.full_like(local, 2.0)
    for i in range(inner - 1, -1, -1):
        if i < inner - 1:
            local = r_local[i] - c_term[i] * local
            prev = r_prev[i] - c_term[i] * prev
            nxt = -c_term[i] * nxt
        base_ref[i] = 2.0 * local - base_ref[i]
        p_ref[i] = 2.0 * prev
        n_ref[i] = 2.0 * nxt
    head_coupling = lower[0]
    own = (
        own_lower,
        own_diag,
        own_right,
        head_coupling * (prev - 1.0),
        head_coupling * nxt,
        head_coupling * local,
    )
    for block in range(pieces_ref.shape[0]):
        for i in range(6):
            pieces_ref[block, i] = own[i]


def depth_local(temp, conduct, downward, from_right, temp_prev, blocks):
    rows, lines, width = temp.shape
    full = jax.ShapeDtypeStruct(temp.shape, temp.dtype)
    copies = jax.ShapeDtypeStruct((blocks, 6, lines, width), temp.dtype)
    return pl.pallas_call(depth_kernel, out_shape=(full, full, full, copies))(
        temp, conduct, downward, from_right, temp_prev
    )


def reduced_solve(copies, ratio, axis):
    line_shape = copies.shape[2:]
    every = lax.all_to_all(copies, axis, 0, 0, tiled=False)
    zero_row = jnp.zeros_like(every[:1, 0])
    from_next = [jnp.concatenate([every[1:, i], zero_row], axis=0) for i in (3, 4, 5)]
    red_diag = every[:, 1] + from_next[0]
    red_upper = from_next[1]
    red_right = every[:, 2] - from_next[2]
    solved = cyclic(every[:, 0], red_diag, red_upper, (red_right,), 0)[0]
    padded = jnp.concatenate([zero_row, solved], axis=0)
    index = lax.axis_index(axis)
    previous = lax.dynamic_slice_in_dim(padded, index, 1, 0)[0]
    interface_value = lax.dynamic_slice_in_dim(padded, index + 1, 1, 0)[0]
    return previous, interface_value


def partition_solve(conduct, first_next, rights, ratio, axis_index, axis):
    count = conduct.shape[axis_index]
    lower_band = -ratio * conduct
    inner_lower = take_rows(lower_band, 0, count - 1, axis_index)
    upper_inner = -ratio * take_rows(conduct, 1, count, axis_index)
    diagonal = 1.0 - inner_lower - upper_inner
    positions = lax.broadcasted_iota(jnp.int32, inner_lower.shape, axis_index)
    first_lower = take_rows(inner_lower, 0, 1, axis_index)
    last_upper = take_rows(upper_inner, count - 2, count - 1, axis_index)
    solve_lower = jnp.where(positions == 0, 0.0, inner_lower)
    solve_upper = jnp.where(positions == count - 2, 0.0, upper_inner)
    from_prev = jnp.where(positions == 0, -first_lower, 0.0)
    from_next = jnp.where(positions == count - 2, -last_upper, 0.0)
    inner_rights = take_rows(rights, 0, count - 1, axis_index)
    factors = cyclic_factors(solve_lower, diagonal, solve_upper, axis_index)
    prev_part = cyclic_apply(factors, from_prev, axis_index)
    next_part = cyclic_apply(factors, from_next, axis_index)
    levels, last_diagonal = factors
    strides = [level[0] for level in levels]
    terms = [level[1:] for level in levels]
    terms, last_diagonal, prev_part, next_part = lax.optimization_barrier(
        (terms, last_diagonal, prev_part, next_part)
    )
    factors = ([(s,) + tuple(t) for s, t in zip(strides, terms)], last_diagonal)
    local_part = cyclic_apply(factors, inner_rights, axis_index)
    tail_local = take_rows(local_part, count - 2, count - 1, axis_index)
    tail_prev = take_rows(prev_part, count - 2, count - 1, axis_index)
    tail_next = take_rows(next_part, count - 2, count - 1, axis_index)
    lower_last = take_rows(lower_band, count - 1, count, axis_index)
    right_last = take_rows(rights, count - 1, count, axis_index)
    head_coupling = take_rows(lower_band, 0, 1, axis_index)
    pieces = jnp.stack(
        [
            lower_last * tail_prev,
            1.0 - lower_last + lower_last * tail_next,
            right_last - lower_last * tail_local,
            head_coupling * (take_rows(prev_part, 0, 1, axis_index) - 1.0),
            head_coupling * take_rows(next_part, 0, 1, axis_index),
            head_coupling * take_rows(local_part, 0, 1, axis_index),
        ]
    )
    blocks = lax.axis_size(axis)
    flat = pieces.reshape(pieces.shape[0], -1)
    copies = jnp.broadcast_to(flat[None], (blocks,) + flat.shape)
    previous, interface_value = reduced_solve(copies, ratio, axis)
    previous = previous.reshape(pieces.shape[1:])
    interface_value = interface_value.reshape(pieces.shape[1:])
    inner_values = local_part + prev_part * previous + next_part * interface_value
    return jnp.concatenate([inner_values, interface_value], axis=axis_index)


def on_device(thermal_state, sideways_face_flux_factor, downward_face_flux_factor):
    width = thermal_state.shape[2]
    count = lax.axis_size("lat")
    right_pairs = [(i, i + 1) for i in range(count - 1)]
    left_pairs = [(i + 1, i) for i in range(count - 1)]
    edge_shape = thermal_state.shape[:2] + (1,)
    first_cols = jnp.stack(
        [thermal_state[:, :, 0].reshape(-1), sideways_face_flux_factor[:, :, 0].reshape(-1)]
    )
    from_right = lax.ppermute(first_cols, "lat", left_pairs).reshape((2,) + edge_shape)
    last_col = thermal_state[:, :, width - 1].reshape(-1)
    from_left = lax.ppermute(last_col, "lat", right_pairs).reshape(edge_shape)
    base, prev_weight, own_weight, pieces = depth_local(
        thermal_state,
        sideways_face_flux_factor,
        downward_face_flux_factor,
        from_right,
        from_left,
        lax.axis_size("depth"),
    )
    previous, interface_value = reduced_solve(pieces, ratio_z, "depth")
    lateral_conduct = lax.optimization_barrier((sideways_face_flux_factor, pieces))[0]
    reflected = base + prev_weight * previous + own_weight * interface_value
    return partition_solve(
        lateral_conduct, None, reflected, sideways_coupling_quotient, 2, "lat"
    )


def solution(mesh):
    in_specs = (P("depth", None, "lat"), P("depth", None, "lat"), P("depth", None, "lat"))
    out_specs = P("depth", None, "lat")
    return jax.shard_map(
        on_device, mesh=mesh, in_specs=in_specs, out_specs=out_specs, check_vma=False
    )
```

```python
import jax
import jax.numpy as jnp
from jax import lax
from jax.sharding import PartitionSpec as P
from jax.experimental import pallas as pl
from jax.experimental.pallas import tpu as pltpu

sideways_coupling_quotient = 20.0
ratio_z = 2000.0


def take_rows(values, start, stop, axis_index):
    return lax.slice_in_dim(values, start, stop, axis=axis_index)


def moved(values, stride, axis_index, filler, forward):
    count = values.shape[axis_index]
    pad_shape = list(values.shape)
    pad_shape[axis_index] = stride
    padding = jnp.full(pad_shape, filler, values.dtype)
    if forward:
        return jnp.concatenate(
            [take_rows(values, stride, count, axis_index), padding], axis=axis_index
        )
    return jnp.concatenate(
        [padding, take_rows(values, 0, count - stride, axis_index)], axis=axis_index
    )


def level_update(lower_band, diagonal, upper_band, rights, below, above):
    alpha_term = -lower_band / below[1]
    gamma_term = -upper_band / above[1]
    new_diagonal = diagonal + alpha_term * below[2] + gamma_term * above[0]
    new_rights = tuple(
        (
            column + alpha_term * low_col + gamma_term * high_col
            for column, low_col, high_col in zip(rights, below[3], above[3])
        )
    )
    return (alpha_term * below[0], new_diagonal, gamma_term * above[2], new_rights)


def cyclic_factors(lower_band, diagonal, upper_band, axis_index):
    count = lower_band.shape[axis_index]
    stride = 1
    levels = []
    while stride < count:
        alpha_term = -lower_band / moved(diagonal, stride, axis_index, 1.0, False)
        gamma_term = -upper_band / moved(diagonal, stride, axis_index, 1.0, True)
        new_diagonal = (
            diagonal
            + alpha_term * moved(upper_band, stride, axis_index, 0.0, False)
            + gamma_term * moved(lower_band, stride, axis_index, 0.0, True)
        )
        lower_band = alpha_term * moved(lower_band, stride, axis_index, 0.0, False)
        upper_band = gamma_term * moved(upper_band, stride, axis_index, 0.0, True)
        diagonal = new_diagonal
        levels.append((stride, alpha_term, gamma_term))
        stride = stride * 2
    return levels, diagonal


def cyclic_apply(factors, column, axis_index):
    levels, diagonal = factors
    for stride, alpha_term, gamma_term in levels:
        column = (
            column
            + alpha_term * moved(column, stride, axis_index, 0.0, False)
            + gamma_term * moved(column, stride, axis_index, 0.0, True)
        )
    return column / diagonal


def cyclic(lower_band, diagonal, upper_band, rights, axis_index):
    factors = cyclic_factors(lower_band, diagonal, upper_band, axis_index)
    return tuple(cyclic_apply(factors, column, axis_index) for column in rights)


def depth_kernel(t_ref, s_ref, d_ref, right_ref, tl_ref, base_ref, p_ref, n_ref, pieces_ref):
    rows, _, width = t_ref.shape
    temp = t_ref[...]
    conduct = s_ref[...]
    lane = lax.broadcasted_iota(jnp.int32, temp.shape, 2)
    last = lane == width - 1
    first = lane == 0
    temp_right = jnp.where(last, right_ref[0][:, :, None], pltpu.roll(temp, width - 1, 2))
    conduct_right = jnp.where(last, right_ref[1][:, :, None], pltpu.roll(conduct, width - 1, 2))
    temp_left = jnp.where(first, tl_ref[...][:, :, None], pltpu.roll(temp, 1, 2))
    base_ref[...] = temp + sideways_coupling_quotient * (
        conduct_right * (temp_right - temp) - conduct * (temp - temp_left)
    )
    inner = rows - 1
    lower = [-ratio_z * d_ref[i] for i in range(rows)]
    upper = [lower[i + 1] for i in range(inner)]
    c_term, r_local, r_prev = [], [], []
    r_next = None
    for i in range(inner):
        diagonal = 1.0 - lower[i] - upper[i]
        rhs = base_ref[i]
        if i == 0:
            den = diagonal
            local = rhs / den
            prev = -lower[i] / den
        else:
            den = diagonal - lower[i] * c_term[i - 1]
            local = (rhs - lower[i] * r_local[i - 1]) / den
            prev = (-lower[i] * r_prev[i - 1]) / den
        if i < inner - 1:
            c_term.append(upper[i] / den)
        else:
            c_term.append(None)
            r_next = -upper[i] / den
        r_local.append(local)
        r_prev.append(prev)
    local = r_local[inner - 1]
    prev = r_prev[inner - 1]
    nxt = r_next
    lower_last = lower[rows - 1]
    right_last = base_ref[rows - 1]
    own_lower = lower_last * prev
    own_diag = 1.0 - lower_last + lower_last * nxt
    own_right = right_last - lower_last * local
    base_ref[rows - 1] = -right_last
    p_ref[rows - 1] = jnp.zeros_like(local)
    n_ref[rows - 1] = jnp.full_like(local, 2.0)
    for i in range(inner - 1, -1, -1):
        if i < inner - 1:
            local = r_local[i] - c_term[i] * local
            prev = r_prev[i] - c_term[i] * prev
            nxt = -c_term[i] * nxt
        base_ref[i] = 2.0 * local - base_ref[i]
        p_ref[i] = 2.0 * prev
        n_ref[i] = 2.0 * nxt
    head_coupling = lower[0]
    own = (
        own_lower,
        own_diag,
        own_right,
        head_coupling * (prev - 1.0),
        head_coupling * nxt,
        head_coupling * local,
    )
    for block in range(pieces_ref.shape[0]):
        for i in range(6):
            pieces_ref[block, i] = own[i]


def depth_local(temp, conduct, downward, from_right, temp_prev, blocks):
    rows, lines, width = temp.shape
    full = jax.ShapeDtypeStruct(temp.shape, temp.dtype)
    copies = jax.ShapeDtypeStruct((blocks, 6, lines, width), temp.dtype)
    return pl.pallas_call(depth_kernel, out_shape=(full, full, full, copies))(
        temp, conduct, downward, from_right, temp_prev
    )


def reduced_solve(copies, ratio, axis):
    line_shape = copies.shape[2:]
    every = lax.all_to_all(copies, axis, 0, 0, tiled=False)
    zero_row = jnp.zeros_like(every[:1, 0])
    from_next = [jnp.concatenate([every[1:, i], zero_row], axis=0) for i in (3, 4, 5)]
    red_diag = every[:, 1] + from_next[0]
    red_upper = from_next[1]
    red_right = every[:, 2] - from_next[2]
    solved = cyclic(every[:, 0], red_diag, red_upper, (red_right,), 0)[0]
    padded = jnp.concatenate([zero_row, solved], axis=0)
    index = lax.axis_index(axis)
    previous = lax.dynamic_slice_in_dim(padded, index, 1, 0)[0]
    interface_value = lax.dynamic_slice_in_dim(padded, index + 1, 1, 0)[0]
    return previous, interface_value


def partition_solve(conduct, first_next, rights, ratio, axis_index, axis):
    count = conduct.shape[axis_index]
    lower_band = -ratio * conduct
    inner_lower = take_rows(lower_band, 0, count - 1, axis_index)
    upper_inner = -ratio * take_rows(conduct, 1, count, axis_index)
    diagonal = 1.0 - inner_lower - upper_inner
    positions = lax.broadcasted_iota(jnp.int32, inner_lower.shape, axis_index)
    first_lower = take_rows(inner_lower, 0, 1, axis_index)
    last_upper = take_rows(upper_inner, count - 2, count - 1, axis_index)
    solve_lower = jnp.where(positions == 0, 0.0, inner_lower)
    solve_upper = jnp.where(positions == count - 2, 0.0, upper_inner)
    from_prev = jnp.where(positions == 0, -first_lower, 0.0)
    from_next = jnp.where(positions == count - 2, -last_upper, 0.0)
    inner_rights = take_rows(rights, 0, count - 1, axis_index)
    factors = cyclic_factors(solve_lower, diagonal, solve_upper, axis_index)
    prev_part = cyclic_apply(factors, from_prev, axis_index)
    next_part = cyclic_apply(factors, from_next, axis_index)
    levels, last_diagonal = factors
    strides = [level[0] for level in levels]
    terms = [level[1:] for level in levels]
    terms, last_diagonal, prev_part, next_part = lax.optimization_barrier(
        (terms, last_diagonal, prev_part, next_part)
    )
    factors = ([(s,) + tuple(t) for s, t in zip(strides, terms)], last_diagonal)
    local_part = cyclic_apply(factors, inner_rights, axis_index)
    tail_local = take_rows(local_part, count - 2, count - 1, axis_index)
    tail_prev = take_rows(prev_part, count - 2, count - 1, axis_index)
    tail_next = take_rows(next_part, count - 2, count - 1, axis_index)
    lower_last = take_rows(lower_band, count - 1, count, axis_index)
    right_last = take_rows(rights, count - 1, count, axis_index)
    head_coupling = take_rows(lower_band, 0, 1, axis_index)
    pieces = jnp.stack(
        [
            lower_last * tail_prev,
            1.0 - lower_last + lower_last * tail_next,
            right_last - lower_last * tail_local,
            head_coupling * (take_rows(prev_part, 0, 1, axis_index) - 1.0),
            head_coupling * take_rows(next_part, 0, 1, axis_index),
            head_coupling * take_rows(local_part, 0, 1, axis_index),
        ]
    )
    blocks = lax.axis_size(axis)
    flat = pieces.reshape(pieces.shape[0], -1)
    copies = jnp.broadcast_to(flat[None], (blocks,) + flat.shape)
    previous, interface_value = reduced_solve(copies, ratio, axis)
    previous = previous.reshape(pieces.shape[1:])
    interface_value = interface_value.reshape(pieces.shape[1:])
    inner_values = local_part + prev_part * previous + next_part * interface_value
    return jnp.concatenate([inner_values, interface_value], axis=axis_index)


def on_device(thermal_state, sideways_face_flux_factor, downward_face_flux_factor):
    width = thermal_state.shape[2]
    count = lax.axis_size("lat")
    right_pairs = [(i, i + 1) for i in range(count - 1)]
    left_pairs = [(i + 1, i) for i in range(count - 1)]
    edge_shape = thermal_state.shape[:2]
    first_cols = jnp.stack(
        [thermal_state[:, :, 0].reshape(-1), sideways_face_flux_factor[:, :, 0].reshape(-1)]
    )
    from_right = lax.ppermute(first_cols, "lat", left_pairs).reshape((2,) + edge_shape)
    last_col = thermal_state[:, :, width - 1].reshape(-1)
    from_left = lax.ppermute(last_col, "lat", right_pairs).reshape(edge_shape)
    base, prev_weight, own_weight, pieces = depth_local(
        thermal_state,
        sideways_face_flux_factor,
        downward_face_flux_factor,
        from_right,
        from_left,
        lax.axis_size("depth"),
    )
    previous, interface_value = reduced_solve(pieces, ratio_z, "depth")
    lateral_conduct = lax.optimization_barrier((sideways_face_flux_factor, pieces))[0]
    reflected = base + prev_weight * previous + own_weight * interface_value
    return partition_solve(
        lateral_conduct, None, reflected, sideways_coupling_quotient, 2, "lat"
    )


def solution(mesh):
    in_specs = (P("depth", None, "lat"), P("depth", None, "lat"), P("depth", None, "lat"))
    out_specs = P("depth", None, "lat")
    return jax.shard_map(
        on_device, mesh=mesh, in_specs=in_specs, out_specs=out_specs, check_vma=False
    )
```
